1024 devices in a mesh: frames: 64 (over z, core), rows: 16 (over y, x).
Axes of the slice: x: 4, y: 4, z: 32, core: 2. Of those that a mesh axis runs over, the one named last changes fastest.
Arguments:
- images: float32 [128, 32, 96, 128], P('frames', 'rows'), may hold values from -6 to 6
- spatial_weight: float32 [3, 3, 128, 128], replicated, may hold values from -0.1875 to 0.1875
- temporal_weight: float32 [3, 128, 128], replicated, may hold values from -0.3125 to 0.3125
- cotangent: float32 [128, 32, 96, 128], P('frames', 'rows'), may hold values from -6 to 6
Outputs:
- block_out: float32 [128, 32, 96, 128], P('frames', 'rows')
- grad_images: float32 [128, 32, 96, 128], P('frames', 'rows')
- grad_spatial: float32 [3, 3, 128, 128], P(None, None, None, 'rows')
- grad_temporal: float32 [3, 128, 128], P(None, None, 'rows')
The draws below stay inside these ranges and needn't reach their ends.
All inputs are finite; a program needn't handle non-finite values.
Results may differ from the reference program's by a relative error of at most 0.0003.
Values sent between devices are 32-bit elements; how exact they have to be, the bound alone decides.
No kernel may reach another device: no remote copies, remote signals or barrier semaphores. Data moves between devices by JAX's collectives and lax.ppermute only.
A program may use at most 32 MiB of HBM per device.

```python
import math
import jax
import jax.numpy as jnp
from jax import lax

C = 128
W = 96
FRAMES = 128
HEIGHT = 32


def shard_levels(own_key, dims, split, low, high):
    def one(position, shards_of):
        steps = jax.random.uniform(jax.random.fold_in(jax.random.fold_in(own_key, 6), position), (shards_of,), jnp.float32, low / len(split), high / len(split))
        return jnp.repeat(jnp.exp(steps), dims[position] // shards_of).reshape((-1,) + (1,) * (len(dims) - position - 1))

    factor_of = one(*split[0])
    for cut in split[1:]:
        factor_of = factor_of * one(*cut)
    return factor_of


def centred(own_key, dims, deviation, most, pieces=(), kind=jnp.bfloat16):
    result = deviation * jax.random.normal(own_key, dims, jnp.float32)
    if pieces:
        result = result * shard_levels(own_key, dims, pieces, -0.22, 0.18)
    return jnp.clip(result, -most, most).astype(kind)


def setup_inputs(seed: int = 0) -> dict:
    keys = jax.random.split(jax.random.key(seed), 5)
    images = centred(keys[0], (FRAMES, HEIGHT, W, C), 1.0, 6.0, ((0, 64), (1, 16)), jnp.float32)
    spatial_weight = centred(keys[1], (3, 3, C, C), (9 * C) ** -0.5, 0.1875, (), jnp.float32)
    temporal_weight = centred(keys[2], (3, C, C), (3 * C) ** -0.5, 0.3125, (), jnp.float32)
    cotangent = centred(keys[3], (FRAMES, HEIGHT, W, C), 1.0, 6.0, ((0, 64), (1, 16)), jnp.float32)
    return {"images": images, "spatial_weight": spatial_weight, "temporal_weight": temporal_weight, "cotangent": cotangent}


HIGH = lax.Precision.HIGHEST

def spatial(frame, kernel):
    height, width = (frame.shape[0], frame.shape[1])
    padded = jnp.pad(frame, ((1, 1), (1, 1), (0, 0)))
    total = jnp.zeros(frame.shape, jnp.float32)
    for i in range(3):
        for j in range(3):
            total = total + jnp.einsum('hwc,cd->hwd', padded[i:i + height, j:j + width], kernel[i, j], precision=HIGH)
    return total

def spatial_back(grad, kernel):
    height, width = (grad.shape[0], grad.shape[1])
    padded = jnp.pad(grad, ((1, 1), (1, 1), (0, 0)))
    total = jnp.zeros(grad.shape, jnp.float32)
    for i in range(3):
        for j in range(3):
            total = total + jnp.einsum('hwd,cd->hwc', padded[2 - i:2 - i + height, 2 - j:2 - j + width], kernel[i, j], precision=HIGH)
    return total

def kernel_terms(frame, grad):
    height, width = (frame.shape[0], frame.shape[1])
    padded = jnp.pad(frame, ((1, 1), (1, 1), (0, 0)))
    rows_out = []
    for i in range(3):
        cols_out = []
        for j in range(3):
            cols_out.append(jnp.einsum('hwc,hwd->cd', padded[i:i + height, j:j + width], grad, precision=HIGH))
        rows_out.append(jnp.stack(cols_out))
    return jnp.stack(rows_out)

def reference(images, spatial_weight, temporal_weight, cotangent):
    nframes, height, width, chans = images.shape
    pre = lax.map(lambda frame: spatial(frame, spatial_weight), images)

    def fetch(array, index):
        safe = jnp.clip(index, 0, nframes - 1).astype(jnp.int32)
        valid = jnp.logical_and(index >= 0, index < nframes)
        return jnp.where(valid, lax.dynamic_index_in_dim(array, safe, 0, keepdims=False), jnp.zeros((height, width, chans), jnp.float32))

    def activ(value):
        return value * jax.nn.sigmoid(value)

    def step(carry, index):
        acc_s, acc_t = carry
        pre_now = fetch(pre, index)
        sig = jax.nn.sigmoid(pre_now)
        lagged = [activ(pre_now), activ(fetch(pre, index - 1)), activ(fetch(pre, index - 2))]
        grads = [fetch(cotangent, index), fetch(cotangent, index + 1), fetch(cotangent, index + 2)]
        mixed = jnp.zeros((height, width, chans), jnp.float32)
        dact = jnp.zeros((height, width, chans), jnp.float32)
        for k in range(3):
            mixed = mixed + jnp.einsum('hwc,cd->hwd', lagged[k], temporal_weight[k], precision=HIGH)
            dact = dact + jnp.einsum('hwd,cd->hwc', grads[k], temporal_weight[k], precision=HIGH)
        out_now = fetch(images, index) + mixed
        dpre = dact * sig * (1.0 + pre_now * (1.0 - sig))
        gimg = grads[0] + spatial_back(dpre, spatial_weight)
        acc_s = acc_s + kernel_terms(fetch(images, index), dpre)
        acc_t = acc_t + jnp.stack([jnp.einsum('hwc,hwd->cd', lagged[k], grads[0], precision=HIGH) for k in range(3)])
        return ((acc_s, acc_t), (out_now, gimg))
    start = (jnp.zeros((3, 3, chans, chans), jnp.float32), jnp.zeros((3, chans, chans), jnp.float32))
    (acc_s, acc_t), (block_out, grad_images) = lax.scan(step, start, jnp.arange(nframes, dtype=jnp.int32))
    factor = 1.0 / math.sqrt(nframes * height * width)
    return (block_out, grad_images, acc_s * factor, acc_t * factor)
```

```python
import math

import jax
import jax.numpy as jnp
from jax import lax
from jax.sharding import PartitionSpec as P

HIGH = lax.Precision.HIGHEST


def padded_2(value, sides, width):
    for axis, dim in sides:
        count, length = (lax.axis_size(axis), value.shape[dim])
        up = [(i, (i + 1) % count) for i in range(count - 1)]
        down = [(j, i) for i, j in up]
        last = lax.slice_in_dim(value, length - width, length, axis=dim)
        leading = lax.slice_in_dim(value, 0, width, axis=dim)
        before = lax.ppermute(last, axis, up)
        after = lax.ppermute(leading, axis, down)
        value = jnp.concatenate([before, value, after], axis=dim)
    return value


def passed_along(value, axis, by):
    count = lax.axis_size(axis)
    pairs = [(i, i + by) for i in range(count) if 0 <= i + by < count]
    return lax.ppermute(value, axis, pairs)


def widen(array):
    return jnp.pad(array, ((0, 0), (0, 0), (1, 1), (0, 0)))


def convolve(source, kernel, height, width):
    total = jnp.zeros((source.shape[0], height, width, kernel.shape[3]), jnp.float32)
    for i in range(3):
        for j in range(3):
            total = total + jnp.einsum(
                "frwc,cd->frwd",
                source[:, i : i + height, j : j + width],
                kernel[i, j],
                precision=HIGH,
            )
    return total


def temporal_back(grad_long, temporal_weight, nframes):
    dact = jnp.zeros((nframes,) + grad_long.shape[1:], jnp.float32)
    for k in range(3):
        dact = dact + jnp.einsum(
            "frwd,cd->frwc", grad_long[k : k + nframes], temporal_weight[k], precision=HIGH
        )
    return dact


def halving_scatter(blocks, axis):
    count = blocks.shape[0]
    me = lax.axis_index(axis)
    mask = count // 2
    while mask >= 1:
        half = blocks.shape[0] // 2
        bit = (me // mask) % 2
        keep = lax.dynamic_slice_in_dim(blocks, bit * half, half, axis=0)
        give = lax.dynamic_slice_in_dim(blocks, (1 - bit) * half, half, axis=0)
        pairs = [(i, i ^ mask) for i in range(count)]
        blocks = keep + lax.ppermute(give, axis, pairs)
        mask //= 2
    return blocks


def doubling_sum(value, axis):
    count = lax.axis_size(axis)
    mask = 1
    while mask < count:
        pairs = [(i, i ^ mask) for i in range(count)]
        value = value + lax.ppermute(value, axis, pairs)
        mask *= 2
    return value


def per_device(images, spatial_weight, temporal_weight, cotangent):
    nframes, strip, width, chans = images.shape
    padded = widen(padded_2(images, (("rows", 1),), 1))
    pre = convolve(padded, spatial_weight, strip, width)
    sig = jax.nn.sigmoid(pre)
    later = passed_along(cotangent, "frames", -1)
    grad_long = jnp.concatenate([cotangent, later], axis=0)
    dact = temporal_back(grad_long, temporal_weight, nframes)
    dpre = dact * sig * (1.0 + pre * (1.0 - sig))
    dpre_wide = widen(padded_2(dpre, (("rows", 1),), 1))
    act = pre * sig
    earlier = passed_along(act, "frames", 1)
    longer = jnp.concatenate([earlier, act], axis=0)
    mixed = jnp.zeros(images.shape, jnp.float32)
    for k in range(3):
        mixed = mixed + jnp.einsum(
            "frwc,cd->frwd", longer[2 - k : 2 - k + nframes], temporal_weight[k], precision=HIGH
        )
    block_out = images + mixed
    grad_images = cotangent
    for i in range(3):
        for j in range(3):
            grad_images = grad_images + jnp.einsum(
                "frwd,cd->frwc",
                dpre_wide[:, 2 - i : 2 - i + strip, 2 - j : 2 - j + width],
                spatial_weight[i, j],
                precision=HIGH,
            )
    total_cells = nframes * lax.axis_size("frames") * strip * lax.axis_size("rows") * width
    factor = 1.0 / math.sqrt(total_cells)
    taps = []
    for i in range(3):
        for j in range(3):
            taps.append(
                jnp.einsum(
                    "frwc,frwd->dc", padded[:, i : i + strip, j : j + width], dpre, precision=HIGH
                )
            )
    for k in range(3):
        taps.append(
            jnp.einsum("frwc,frwd->dc", longer[2 - k : 2 - k + nframes], cotangent, precision=HIGH)
        )
    nrows = lax.axis_size("rows")
    terms = jnp.stack(taps, axis=1) * factor
    terms = terms.reshape(nrows, chans // nrows, len(taps), chans)
    summed = halving_scatter(terms, "rows")[0]
    summed = doubling_sum(summed, "frames")
    summed = jnp.transpose(summed, (1, 2, 0))
    grad_spatial = summed[:9].reshape(3, 3, chans, summed.shape[2])
    grad_temporal = summed[9:]
    return (block_out, grad_images, grad_spatial, grad_temporal)


def solution(mesh):
    return jax.shard_map(
        per_device,
        mesh=mesh,
        in_specs=(P("frames", "rows", None, None), P(), P(), P("frames", "rows", None, None)),
        out_specs=(
            P("frames", "rows", None, None),
            P("frames", "rows", None, None),
            P(None, None, None, "rows"),
            P(None, None, "rows"),
        ),
        check_vma=False,
    )
```

```python
import math

import jax
import jax.numpy as jnp
from jax import lax
from jax.sharding import PartitionSpec as P

HIGH = lax.Precision.HIGHEST


def padded_2(value, sides, width):
    for axis, dim in sides:
        count, length = (lax.axis_size(axis), value.shape[dim])
        up = [(i, (i + 1) % count) for i in range(count - 1)]
        down = [(j, i) for i, j in up]
        last = lax.slice_in_dim(value, length - width, length, axis=dim)
        leading = lax.slice_in_dim(value, 0, width, axis=dim)
        before = lax.ppermute(last, axis, up)
        after = lax.ppermute(leading, axis, down)
        value = jnp.concatenate([before, value, after], axis=dim)
    return value


def passed_along(value, axis, by):
    count = lax.axis_size(axis)
    pairs = [(i, i + by) for i in range(count) if 0 <= i + by < count]
    return lax.ppermute(value, axis, pairs)


def widen(array):
    return jnp.pad(array, ((0, 0), (0, 0), (1, 1), (0, 0)))


def convolve(source, kernel, height, width):
    total = jnp.zeros((source.shape[0], height, width, kernel.shape[3]), jnp.float32)
    for i in range(3):
        for j in range(3):
            total = total + jnp.einsum(
                "frwc,cd->frwd",
                source[:, i : i + height, j : j + width],
                kernel[i, j],
                precision=HIGH,
            )
    return total


def temporal_back(grad_long, temporal_weight, nframes):
    dact = jnp.zeros((nframes,) + grad_long.shape[1:], jnp.float32)
    for k in range(3):
        dact = dact + jnp.einsum(
            "frwd,cd->frwc", grad_long[k : k + nframes], temporal_weight[k], precision=HIGH
        )
    return dact


def halving_scatter(blocks, axis, order):
    count = lax.axis_size(axis)
    bits = count.bit_length() - 1
    me = lax.axis_index(axis)
    rest = blocks.shape[1:]
    blocks = blocks.reshape((2,) * bits + rest)
    for mask in order:
        dim = bits - mask.bit_length()
        bit = (me // mask) % 2
        keep = lax.dynamic_slice_in_dim(blocks, bit, 1, axis=dim)
        give = lax.dynamic_slice_in_dim(blocks, 1 - bit, 1, axis=dim)
        pairs = [(i, i ^ mask) for i in range(count)]
        blocks = keep + lax.ppermute(give, axis, pairs)
    return blocks.reshape(rest)


def doubling_sum(value, axis, first):
    count = lax.axis_size(axis)
    mask = first
    while mask < count:
        pairs = [(i, i ^ mask) for i in range(count)]
        value = value + lax.ppermute(value, axis, pairs)
        mask *= 2
    return value


def pair_gather(value, axis):
    count = lax.axis_size(axis)
    low = lax.axis_index(axis) % 2 == 0
    other = lax.ppermute(value, axis, [(i, i ^ 1) for i in range(count)])
    return jnp.where(low, jnp.concatenate([value, other]), jnp.concatenate([other, value]))


def per_device(images, spatial_weight, temporal_weight, cotangent):
    nframes, strip, width, chans = images.shape
    padded = widen(padded_2(images, (("rows", 1),), 1))
    pre = convolve(padded, spatial_weight, strip, width)
    sig = jax.nn.sigmoid(pre)
    later = passed_along(cotangent, "frames", -1)
    grad_long = jnp.concatenate([cotangent, later], axis=0)
    dact = temporal_back(grad_long, temporal_weight, nframes)
    dpre = dact * sig * (1.0 + pre * (1.0 - sig))
    dpre_wide = widen(padded_2(dpre, (("rows", 1),), 1))
    act = pre * sig
    earlier = passed_along(act, "frames", 1)
    longer = jnp.concatenate([earlier, act], axis=0)
    mixed = jnp.zeros(images.shape, jnp.float32)
    for k in range(3):
        mixed = mixed + jnp.einsum(
            "frwc,cd->frwd", longer[2 - k : 2 - k + nframes], temporal_weight[k], precision=HIGH
        )
    block_out = images + mixed
    grad_images = cotangent
    for i in range(3):
        for j in range(3):
            grad_images = grad_images + jnp.einsum(
                "frwd,cd->frwc",
                dpre_wide[:, 2 - i : 2 - i + strip, 2 - j : 2 - j + width],
                spatial_weight[i, j],
                precision=HIGH,
            )
    total_cells = nframes * lax.axis_size("frames") * strip * lax.axis_size("rows") * width
    factor = 1.0 / math.sqrt(total_cells)
    taps = []
    for i in range(3):
        for j in range(3):
            taps.append(
                jnp.einsum(
                    "frwc,frwd->dc", padded[:, i : i + strip, j : j + width], dpre, precision=HIGH
                )
            )
    for k in range(3):
        taps.append(
            jnp.einsum("frwc,frwd->dc", longer[2 - k : 2 - k + nframes], cotangent, precision=HIGH)
        )
    nrows = lax.axis_size("rows")
    terms = jnp.stack(taps, axis=1) * factor
    terms = terms.reshape(nrows, 2, chans // nrows // 2, len(taps), chans)
    parity = lax.axis_index("frames") % 2
    keep = lax.dynamic_index_in_dim(terms, parity, axis=1, keepdims=False)
    give = lax.dynamic_index_in_dim(terms, 1 - parity, axis=1, keepdims=False)
    nframes_all = lax.axis_size("frames")
    terms = keep + lax.ppermute(give, "frames", [(i, i ^ 1) for i in range(nframes_all)])
    order = [nrows // 4, 1, nrows // 2, 2] if nrows == 16 else [nrows >> k for k in range(1, 5)]
    terms = halving_scatter(terms, "rows", [m for m in order if m >= 1])
    summed = pair_gather(doubling_sum(terms, "frames", 2), "frames")
    summed = jnp.transpose(summed, (1, 2, 0))
    grad_spatial = summed[:9].reshape(3, 3, chans, summed.shape[2])
    grad_temporal = summed[9:]
    return (block_out, grad_images, grad_spatial, grad_temporal)


def solution(mesh):
    return jax.shard_map(
        per_device,
        mesh=mesh,
        in_specs=(P("frames", "rows", None, None), P(), P(), P("frames", "rows", None, None)),
        out_specs=(
            P("frames", "rows", None, None),
            P("frames", "rows", None, None),
            P(None, None, None, "rows"),
            P(None, None, "rows"),
        ),
        check_vma=False,
    )
```

```python
import math

import jax
import jax.numpy as jnp
from jax import lax
from jax.sharding import PartitionSpec as P

HIGH = lax.Precision.HIGHEST


def padded_2(value, sides, width):
    for axis, dim in sides:
        count, length = (lax.axis_size(axis), value.shape[dim])
        up = [(i, (i + 1) % count) for i in range(count - 1)]
        down = [(j, i) for i, j in up]
        last = lax.slice_in_dim(value, length - width, length, axis=dim)
        leading = lax.slice_in_dim(value, 0, width, axis=dim)
        before = lax.ppermute(last, axis, up)
        after = lax.ppermute(leading, axis, down)
        value = jnp.concatenate([before, value, after], axis=dim)
    return value


def passed_along(value, axis, by):
    count = lax.axis_size(axis)
    pairs = [(i, i + by) for i in range(count) if 0 <= i + by < count]
    return lax.ppermute(value, axis, pairs)


def widen(array):
    return jnp.pad(array, ((0, 0), (0, 0), (1, 1), (0, 0)))


def convolve(source, kernel, height, width):
    total = jnp.zeros((source.shape[0], height, width, kernel.shape[3]), jnp.float32)
    for i in range(3):
        for j in range(3):
            total = total + jnp.einsum(
                "frwc,cd->frwd",
                source[:, i : i + height, j : j + width],
                kernel[i, j],
                precision=HIGH,
            )
    return total


def temporal_back(grad_long, temporal_weight, nframes):
    dact = jnp.zeros((nframes,) + grad_long.shape[1:], jnp.float32)
    for k in range(3):
        dact = dact + jnp.einsum(
            "frwd,cd->frwc", grad_long[k : k + nframes], temporal_weight[k], precision=HIGH
        )
    return dact


def halving_scatter(blocks, axis, order):
    count = lax.axis_size(axis)
    bits = count.bit_length() - 1
    me = lax.axis_index(axis)
    rest = blocks.shape[1:]
    blocks = blocks.reshape((2,) * bits + rest)
    for mask in order:
        dim = bits - mask.bit_length()
        bit = (me // mask) % 2
        keep = lax.dynamic_slice_in_dim(blocks, bit, 1, axis=dim)
        give = lax.dynamic_slice_in_dim(blocks, 1 - bit, 1, axis=dim)
        pairs = [(i, i ^ mask) for i in range(count)]
        blocks = keep + lax.ppermute(give, axis, pairs)
    return blocks.reshape(rest)


def doubling_sum(value, axis, first):
    count = lax.axis_size(axis)
    mask = first
    while mask < count // 2:
        pairs = [(i, i ^ mask) for i in range(count)]
        value = value + lax.ppermute(value, axis, pairs)
        mask *= 2
    pairs = [(i, count - first * (i // first + 1) + i % first) for i in range(count)]
    return value + lax.ppermute(value, axis, pairs)


def pair_gather(value, axis):
    count = lax.axis_size(axis)
    low = lax.axis_index(axis) % 2 == 0
    other = lax.ppermute(value, axis, [(i, i ^ 1) for i in range(count)])
    return jnp.where(low, jnp.concatenate([value, other]), jnp.concatenate([other, value]))


def per_device(images, spatial_weight, temporal_weight, cotangent):
    nframes, strip, width, chans = images.shape
    padded = widen(padded_2(images, (("rows", 1),), 1))
    pre = convolve(padded, spatial_weight, strip, width)
    sig = jax.nn.sigmoid(pre)
    later = passed_along(cotangent, "frames", -1)
    grad_long = jnp.concatenate([cotangent, later], axis=0)
    dact = temporal_back(grad_long, temporal_weight, nframes)
    dpre = dact * sig * (1.0 + pre * (1.0 - sig))
    dpre_wide = widen(padded_2(dpre, (("rows", 1),), 1))
    act = pre * sig
    earlier = passed_along(act, "frames", 1)
    longer = jnp.concatenate([earlier, act], axis=0)
    mixed = jnp.zeros(images.shape, jnp.float32)
    for k in range(3):
        mixed = mixed + jnp.einsum(
            "frwc,cd->frwd", longer[2 - k : 2 - k + nframes], temporal_weight[k], precision=HIGH
        )
    block_out = images + mixed
    grad_images = cotangent
    for i in range(3):
        for j in range(3):
            grad_images = grad_images + jnp.einsum(
                "frwd,cd->frwc",
                dpre_wide[:, 2 - i : 2 - i + strip, 2 - j : 2 - j + width],
                spatial_weight[i, j],
                precision=HIGH,
            )
    total_cells = nframes * lax.axis_size("frames") * strip * lax.axis_size("rows") * width
    factor = 1.0 / math.sqrt(total_cells)
    taps = []
    for i in range(3):
        for j in range(3):
            taps.append(
                jnp.einsum(
                    "frwc,frwd->dc", padded[:, i : i + strip, j : j + width], dpre, precision=HIGH
                )
            )
    for k in range(3):
        taps.append(
            jnp.einsum("frwc,frwd->dc", longer[2 - k : 2 - k + nframes], cotangent, precision=HIGH)
        )
    nrows = lax.axis_size("rows")
    terms = jnp.stack(taps, axis=1) * factor
    terms = terms.reshape(nrows, 2, chans // nrows // 2, len(taps), chans)
    parity = lax.axis_index("frames") % 2
    keep = lax.dynamic_index_in_dim(terms, parity, axis=1, keepdims=False)
    give = lax.dynamic_index_in_dim(terms, 1 - parity, axis=1, keepdims=False)
    nframes_all = lax.axis_size("frames")
    terms = keep + lax.ppermute(give, "frames", [(i, i ^ 1) for i in range(nframes_all)])
    terms = lax.all_to_all(terms, "rows", 0, 0, tiled=True).sum(axis=0)
    summed = pair_gather(doubling_sum(terms, "frames", 2), "frames")
    summed = jnp.transpose(summed, (1, 2, 0))
    grad_spatial = summed[:9].reshape(3, 3, chans, summed.shape[2])
    grad_temporal = summed[9:]
    return (block_out, grad_images, grad_spatial, grad_temporal)


def solution(mesh):
    return jax.shard_map(
        per_device,
        mesh=mesh,
        in_specs=(P("frames", "rows", None, None), P(), P(), P("frames", "rows", None, None)),
        out_specs=(
            P("frames", "rows", None, None),
            P("frames", "rows", None, None),
            P(None, None, None, "rows"),
            P(None, None, "rows"),
        ),
        check_vma=False,
    )
```

```python
import math

import jax
import jax.numpy as jnp
from jax import lax
from jax.sharding import PartitionSpec as P

HIGH = lax.Precision.HIGHEST


def padded_2(value, sides, width):
    for axis, dim in sides:
        count, length = (lax.axis_size(axis), value.shape[dim])
        up = [(i, (i + 1) % count) for i in range(count - 1)]
        down = [(j, i) for i, j in up]
        last = lax.slice_in_dim(value, length - width, length, axis=dim)
        leading = lax.slice_in_dim(value, 0, width, axis=dim)
        before = lax.ppermute(last, axis, up)
        after = lax.ppermute(leading, axis, down)
        value = jnp.concatenate([before, value, after], axis=dim)
    return value


def passed_along(value, axis, by):
    count = lax.axis_size(axis)
    pairs = [(i, i + by) for i in range(count) if 0 <= i + by < count]
    return lax.ppermute(value, axis, pairs)


def widen(array):
    return jnp.pad(array, ((0, 0), (0, 0), (1, 1), (0, 0)))


def convolve(source, kernel, height, width):
    total = jnp.zeros((source.shape[0], height, width, kernel.shape[3]), jnp.float32)
    for i in range(3):
        for j in range(3):
            total = total + jnp.einsum(
                "frwc,cd->frwd",
                source[:, i : i + height, j : j + width],
                kernel[i, j],
                precision=HIGH,
            )
    return total


def temporal_back(grad_long, temporal_weight, nframes):
    dact = jnp.zeros((nframes,) + grad_long.shape[1:], jnp.float32)
    for k in range(3):
        dact = dact + jnp.einsum(
            "frwd,cd->frwc", grad_long[k : k + nframes], temporal_weight[k], precision=HIGH
        )
    return dact


def halving_scatter(blocks, axis, order):
    count = lax.axis_size(axis)
    bits = count.bit_length() - 1
    me = lax.axis_index(axis)
    rest = blocks.shape[1:]
    blocks = blocks.reshape((2,) * bits + rest)
    for mask in order:
        dim = bits - mask.bit_length()
        bit = (me // mask) % 2
        keep = lax.dynamic_slice_in_dim(blocks, bit, 1, axis=dim)
        give = lax.dynamic_slice_in_dim(blocks, 1 - bit, 1, axis=dim)
        pairs = [(i, i ^ mask) for i in range(count)]
        blocks = keep + lax.ppermute(give, axis, pairs)
    return blocks.reshape(rest)


def doubling_sum(value, axis, first):
    count = lax.axis_size(axis)
    mask = first
    while mask < count // 2:
        pairs = [(i, i ^ mask) for i in range(count)]
        value = value + lax.ppermute(value, axis, pairs)
        mask *= 2
    ring = count // first
    pairs = [(i, first * ring_partner(i // first, ring) + i % first) for i in range(count)]
    return value + lax.ppermute(value, axis, pairs)


def ring_partner(z, ring):
    if ring % 4:
        return ring - 1 - z
    quarter = ring // 4
    shift = (3 * quarter, quarter, -quarter, -3 * quarter)
    return z + shift[z // quarter]


def pair_gather(value, axis):
    count = lax.axis_size(axis)
    low = lax.axis_index(axis) % 2 == 0
    other = lax.ppermute(value, axis, [(i, i ^ 1) for i in range(count)])
    return jnp.where(low, jnp.concatenate([value, other]), jnp.concatenate([other, value]))


def per_device(images, spatial_weight, temporal_weight, cotangent):
    nframes, strip, width, chans = images.shape
    padded = widen(padded_2(images, (("rows", 1),), 1))
    pre = convolve(padded, spatial_weight, strip, width)
    sig = jax.nn.sigmoid(pre)
    later = passed_along(cotangent, "frames", -1)
    grad_long = jnp.concatenate([cotangent, later], axis=0)
    dact = temporal_back(grad_long, temporal_weight, nframes)
    dpre = dact * sig * (1.0 + pre * (1.0 - sig))
    dpre_wide = widen(padded_2(dpre, (("rows", 1),), 1))
    act = pre * sig
    earlier = passed_along(act, "frames", 1)
    longer = jnp.concatenate([earlier, act], axis=0)
    mixed = jnp.zeros(images.shape, jnp.float32)
    for k in range(3):
        mixed = mixed + jnp.einsum(
            "frwc,cd->frwd", longer[2 - k : 2 - k + nframes], temporal_weight[k], precision=HIGH
        )
    block_out = images + mixed
    grad_images = cotangent
    for i in range(3):
        for j in range(3):
            grad_images = grad_images + jnp.einsum(
                "frwd,cd->frwc",
                dpre_wide[:, 2 - i : 2 - i + strip, 2 - j : 2 - j + width],
                spatial_weight[i, j],
                precision=HIGH,
            )
    total_cells = nframes * lax.axis_size("frames") * strip * lax.axis_size("rows") * width
    factor = 1.0 / math.sqrt(total_cells)
    taps = []
    for i in range(3):
        for j in range(3):
            taps.append(
                jnp.einsum(
                    "frwc,frwd->dc", padded[:, i : i + strip, j : j + width], dpre, precision=HIGH
                )
            )
    for k in range(3):
        taps.append(
            jnp.einsum("frwc,frwd->dc", longer[2 - k : 2 - k + nframes], cotangent, precision=HIGH)
        )
    nrows = lax.axis_size("rows")
    terms = jnp.stack(taps, axis=1) * factor
    terms = terms.reshape(nrows, 2, chans // nrows // 2, len(taps), chans)
    parity = lax.axis_index("frames") % 2
    keep = lax.dynamic_index_in_dim(terms, parity, axis=1, keepdims=False)
    give = lax.dynamic_index_in_dim(terms, 1 - parity, axis=1, keepdims=False)
    nframes_all = lax.axis_size("frames")
    terms = keep + lax.ppermute(give, "frames", [(i, i ^ 1) for i in range(nframes_all)])
    terms = lax.all_to_all(terms, "rows", 0, 0, tiled=True).sum(axis=0)
    summed = pair_gather(doubling_sum(terms, "frames", 2), "frames")
    summed = jnp.transpose(summed, (1, 2, 0))
    grad_spatial = summed[:9].reshape(3, 3, chans, summed.shape[2])
    grad_temporal = summed[9:]
    return (block_out, grad_images, grad_spatial, grad_temporal)


def solution(mesh):
    return jax.shard_map(
        per_device,
        mesh=mesh,
        in_specs=(P("frames", "rows", None, None), P(), P(), P("frames", "rows", None, None)),
        out_specs=(
            P("frames", "rows", None, None),
            P("frames", "rows", None, None),
            P(None, None, None, "rows"),
            P(None, None, "rows"),
        ),
        check_vma=False,
    )
```

```python
import math

import jax
import jax.numpy as jnp
from jax import lax
from jax.sharding import PartitionSpec as P

HIGH = lax.Precision.HIGHEST


def padded_2(value, sides, width):
    for axis, dim in sides:
        count, length = (lax.axis_size(axis), value.shape[dim])
        up = [(i, (i + 1) % count) for i in range(count - 1)]
        down = [(j, i) for i, j in up]
        last = lax.slice_in_dim(value, length - width, length, axis=dim)
        leading = lax.slice_in_dim(value, 0, width, axis=dim)
        before = lax.ppermute(last, axis, up)
        after = lax.ppermute(leading, axis, down)
        value = jnp.concatenate([before, value, after], axis=dim)
    return value


def passed_along(value, axis, by):
    count = lax.axis_size(axis)
    pairs = [(i, i + by) for i in range(count) if 0 <= i + by < count]
    return lax.ppermute(value, axis, pairs)


def widen(array):
    return jnp.pad(array, ((0, 0), (0, 0), (1, 1), (0, 0)))


def convolve(source, kernel, height, width):
    total = jnp.zeros((source.shape[0], height, width, kernel.shape[3]), jnp.float32)
    for i in range(3):
        for j in range(3):
            total = total + jnp.einsum(
                "frwc,cd->frwd",
                source[:, i : i + height, j : j + width],
                kernel[i, j],
                precision=HIGH,
            )
    return total


def temporal_back(grad_long, temporal_weight, nframes):
    dact = jnp.zeros((nframes,) + grad_long.shape[1:], jnp.float32)
    for k in range(3):
        dact = dact + jnp.einsum(
            "frwd,cd->frwc", grad_long[k : k + nframes], temporal_weight[k], precision=HIGH
        )
    return dact


def halving_scatter(blocks, axis, order):
    count = lax.axis_size(axis)
    bits = count.bit_length() - 1
    me = lax.axis_index(axis)
    rest = blocks.shape[1:]
    blocks = blocks.reshape((2,) * bits + rest)
    for mask in order:
        dim = bits - mask.bit_length()
        bit = (me // mask) % 2
        keep = lax.dynamic_slice_in_dim(blocks, bit, 1, axis=dim)
        give = lax.dynamic_slice_in_dim(blocks, 1 - bit, 1, axis=dim)
        pairs = [(i, i ^ mask) for i in range(count)]
        blocks = keep + lax.ppermute(give, axis, pairs)
    return blocks.reshape(rest)


def doubling_sum(value, axis, first):
    count = lax.axis_size(axis)
    mask = first
    while mask < count // 2:
        pairs = [(i, i ^ mask) for i in range(count)]
        value = value + lax.ppermute(value, axis, pairs)
        mask *= 2
    ring = count // first
    pairs = [(i, first * ring_partner(i // first, ring) + i % first) for i in range(count)]
    return value + lax.ppermute(value, axis, pairs)


def ring_partner(z, ring):
    if ring % 4:
        return ring - 1 - z
    quarter = ring // 4
    shift = (3 * quarter, quarter, -quarter, -3 * quarter)
    return z + shift[z // quarter]


def pair_gather(value, axis):
    count = lax.axis_size(axis)
    low = lax.axis_index(axis) % 2 == 0
    other = lax.ppermute(value, axis, [(i, i ^ 1) for i in range(count)])
    return jnp.where(low, jnp.concatenate([value, other]), jnp.concatenate([other, value]))


def per_device(images, spatial_weight, temporal_weight, cotangent):
    nframes, strip, width, chans = images.shape
    padded = widen(padded_2(images, (("rows", 1),), 1))
    pre = convolve(padded, spatial_weight, strip, width)
    sig = jax.nn.sigmoid(pre)
    later = passed_along(cotangent, "frames", -1)
    grad_long = jnp.concatenate([cotangent, later], axis=0)
    dact = temporal_back(grad_long, temporal_weight, nframes)
    dpre = dact * sig * (1.0 + pre * (1.0 - sig))
    act = pre * sig
    earlier = passed_along(act, "frames", 1)
    longer = jnp.concatenate([earlier, act], axis=0)
    total_cells = nframes * lax.axis_size("frames") * strip * lax.axis_size("rows") * width
    factor = 1.0 / math.sqrt(total_cells)
    taps = []
    for i in range(3):
        for j in range(3):
            taps.append(
                jnp.einsum(
                    "frwc,frwd->dc", padded[:, i : i + strip, j : j + width], dpre, precision=HIGH
                )
            )
    for k in range(3):
        taps.append(
            jnp.einsum("frwc,frwd->dc", longer[2 - k : 2 - k + nframes], cotangent, precision=HIGH)
        )
    nrows = lax.axis_size("rows")
    terms = jnp.stack(taps, axis=1) * factor
    terms, dpre_late = lax.optimization_barrier((terms, dpre))
    dpre_wide = widen(padded_2(dpre_late, (("rows", 1),), 1))
    mixed = jnp.zeros(images.shape, jnp.float32)
    for k in range(3):
        mixed = mixed + jnp.einsum(
            "frwc,cd->frwd", longer[2 - k : 2 - k + nframes], temporal_weight[k], precision=HIGH
        )
    block_out = images + mixed
    grad_images = cotangent
    for i in range(3):
        for j in range(3):
            grad_images = grad_images + jnp.einsum(
                "frwd,cd->frwc",
                dpre_wide[:, 2 - i : 2 - i + strip, 2 - j : 2 - j + width],
                spatial_weight[i, j],
                precision=HIGH,
            )
    terms = terms.reshape(nrows, 2, chans // nrows // 2, len(taps), chans)
    parity = lax.axis_index("frames") % 2
    keep = lax.dynamic_index_in_dim(terms, parity, axis=1, keepdims=False)
    give = lax.dynamic_index_in_dim(terms, 1 - parity, axis=1, keepdims=False)
    nframes_all = lax.axis_size("frames")
    terms = keep + lax.ppermute(give, "frames", [(i, i ^ 1) for i in range(nframes_all)])
    terms = lax.all_to_all(terms, "rows", 0, 0, tiled=True).sum(axis=0)
    summed = pair_gather(doubling_sum(terms, "frames", 2), "frames")
    summed = jnp.transpose(summed, (1, 2, 0))
    grad_spatial = summed[:9].reshape(3, 3, chans, summed.shape[2])
    grad_temporal = summed[9:]
    return (block_out, grad_images, grad_spatial, grad_temporal)


def solution(mesh):
    return jax.shard_map(
        per_device,
        mesh=mesh,
        in_specs=(P("frames", "rows", None, None), P(), P(), P("frames", "rows", None, None)),
        out_specs=(
            P("frames", "rows", None, None),
            P("frames", "rows", None, None),
            P(None, None, None, "rows"),
            P(None, None, "rows"),
        ),
        check_vma=False,
    )
```

```python
import math

import jax
import jax.numpy as jnp
from jax import lax
from jax.sharding import PartitionSpec as P

HIGH = lax.Precision.HIGHEST


def padded_2(value, sides, width):
    for axis, dim in sides:
        count, length = (lax.axis_size(axis), value.shape[dim])
        up = [(i, (i + 1) % count) for i in range(count - 1)]
        down = [(j, i) for i, j in up]
        last = lax.slice_in_dim(value, length - width, length, axis=dim)
        leading = lax.slice_in_dim(value, 0, width, axis=dim)
        before = lax.ppermute(last, axis, up)
        after = lax.ppermute(leading, axis, down)
        value = jnp.concatenate([before, value, after], axis=dim)
    return value


def passed_along(value, axis, by):
    count = lax.axis_size(axis)
    pairs = [(i, i + by) for i in range(count) if 0 <= i + by < count]
    return lax.ppermute(value, axis, pairs)


def widen(array):
    return jnp.pad(array, ((0, 0), (0, 0), (1, 1), (0, 0)))


def shifted(source, offsets, height, width):
    return jnp.stack([source[:, i : i + height, j : j + width] for i, j in offsets])


def convolve(source, kernel, height, width):
    offsets = [(i, j) for i in range(3) for j in range(3)]
    views = shifted(source, offsets, height, width)
    taps = kernel.reshape(9, kernel.shape[2], kernel.shape[3])
    return jnp.einsum("tfrwc,tcd->frwd", views, taps, precision=HIGH)


def temporal_back(grad_long, temporal_weight, nframes):
    views = jnp.stack([grad_long[k : k + nframes] for k in range(3)])
    return jnp.einsum("kfrwd,kcd->frwc", views, temporal_weight, precision=HIGH)


def halving_scatter(blocks, axis, order):
    count = lax.axis_size(axis)
    bits = count.bit_length() - 1
    me = lax.axis_index(axis)
    rest = blocks.shape[1:]
    blocks = blocks.reshape((2,) * bits + rest)
    for mask in order:
        dim = bits - mask.bit_length()
        bit = (me // mask) % 2
        keep = lax.dynamic_slice_in_dim(blocks, bit, 1, axis=dim)
        give = lax.dynamic_slice_in_dim(blocks, 1 - bit, 1, axis=dim)
        pairs = [(i, i ^ mask) for i in range(count)]
        blocks = keep + lax.ppermute(give, axis, pairs)
    return blocks.reshape(rest)


def doubling_sum(value, axis, first):
    count = lax.axis_size(axis)
    mask = first
    while mask < count // 2:
        pairs = [(i, i ^ mask) for i in range(count)]
        value = value + lax.ppermute(value, axis, pairs)
        mask *= 2
    ring = count // first
    pairs = [(i, first * ring_partner(i // first, ring) + i % first) for i in range(count)]
    return value + lax.ppermute(value, axis, pairs)


def ring_partner(z, ring):
    if ring % 4:
        return ring - 1 - z
    quarter = ring // 4
    shift = (3 * quarter, quarter, -quarter, -3 * quarter)
    return z + shift[z // quarter]


def pair_gather(value, axis):
    count = lax.axis_size(axis)
    low = lax.axis_index(axis) % 2 == 0
    other = lax.ppermute(value, axis, [(i, i ^ 1) for i in range(count)])
    return jnp.where(low, jnp.concatenate([value, other]), jnp.concatenate([other, value]))


def per_device(images, spatial_weight, temporal_weight, cotangent):
    nframes, strip, width, chans = images.shape
    padded = widen(padded_2(images, (("rows", 1),), 1))
    pre = convolve(padded, spatial_weight, strip, width)
    sig = jax.nn.sigmoid(pre)
    later = passed_along(cotangent, "frames", -1)
    grad_long = jnp.concatenate([cotangent, later], axis=0)
    dact = temporal_back(grad_long, temporal_weight, nframes)
    dpre = dact * sig * (1.0 + pre * (1.0 - sig))
    dpre_wide = widen(padded_2(dpre, (("rows", 1),), 1))
    act = pre * sig
    earlier = passed_along(act, "frames", 1)
    longer = jnp.concatenate([earlier, act], axis=0)
    lagged = jnp.stack([longer[2 - k : 2 - k + nframes] for k in range(3)])
    mixed = jnp.einsum("kfrwc,kcd->frwd", lagged, temporal_weight, precision=HIGH)
    block_out = images + mixed
    back = [(2 - i, 2 - j) for i in range(3) for j in range(3)]
    spatial_taps = spatial_weight.reshape(9, chans, chans)
    grad_images = cotangent + jnp.einsum(
        "tfrwd,tcd->frwc", shifted(dpre_wide, back, strip, width), spatial_taps, precision=HIGH
    )
    total_cells = nframes * lax.axis_size("frames") * strip * lax.axis_size("rows") * width
    factor = 1.0 / math.sqrt(total_cells)
    offsets = [(i, j) for i in range(3) for j in range(3)]
    spatial_terms = jnp.einsum(
        "tfrwc,frwd->dtc", shifted(padded, offsets, strip, width), dpre, precision=HIGH
    )
    temporal_terms = jnp.einsum("kfrwc,frwd->dkc", lagged, cotangent, precision=HIGH)
    nrows = lax.axis_size("rows")
    terms = jnp.concatenate([spatial_terms, temporal_terms], axis=1) * factor
    terms = terms.reshape(nrows, 2, chans // nrows // 2, terms.shape[1], chans)
    parity = lax.axis_index("frames") % 2
    keep = lax.dynamic_index_in_dim(terms, parity, axis=1, keepdims=False)
    give = lax.dynamic_index_in_dim(terms, 1 - parity, axis=1, keepdims=False)
    nframes_all = lax.axis_size("frames")
    terms = keep + lax.ppermute(give, "frames", [(i, i ^ 1) for i in range(nframes_all)])
    terms = lax.all_to_all(terms, "rows", 0, 0, tiled=True).sum(axis=0)
    summed = pair_gather(doubling_sum(terms, "frames", 2), "frames")
    summed = jnp.transpose(summed, (1, 2, 0))
    grad_spatial = summed[:9].reshape(3, 3, chans, summed.shape[2])
    grad_temporal = summed[9:]
    return (block_out, grad_images, grad_spatial, grad_temporal)


def solution(mesh):
    return jax.shard_map(
        per_device,
        mesh=mesh,
        in_specs=(P("frames", "rows", None, None), P(), P(), P("frames", "rows", None, None)),
        out_specs=(
            P("frames", "rows", None, None),
            P("frames", "rows", None, None),
            P(None, None, None, "rows"),
            P(None, None, "rows"),
        ),
        check_vma=False,
    )
```

```python
import math

import jax
import jax.numpy as jnp
from jax import lax
from jax.sharding import PartitionSpec as P

HIGH = lax.Precision.HIGHEST


def padded_2(value, sides, width):
    for axis, dim in sides:
        count, length = (lax.axis_size(axis), value.shape[dim])
        up = [(i, (i + 1) % count) for i in range(count - 1)]
        down = [(j, i) for i, j in up]
        last = lax.slice_in_dim(value, length - width, length, axis=dim)
        leading = lax.slice_in_dim(value, 0, width, axis=dim)
        before = lax.ppermute(last, axis, up)
        after = lax.ppermute(leading, axis, down)
        value = jnp.concatenate([before, value, after], axis=dim)
    return value


def passed_along(value, axis, by):
    count = lax.axis_size(axis)
    pairs = [(i, i + by) for i in range(count) if 0 <= i + by < count]
    return lax.ppermute(value, axis, pairs)


def widen(array):
    return jnp.pad(array, ((0, 0), (0, 0), (1, 1), (0, 0)))


def shifted(source, offsets, height, width):
    return jnp.stack([source[:, i : i + height, j : j + width] for i, j in offsets])


def convolve(source, kernel, height, width):
    offsets = [(i, j) for i in range(3) for j in range(3)]
    views = shifted(source, offsets, height, width)
    taps = kernel.reshape(9, kernel.shape[2], kernel.shape[3])
    return jnp.einsum("tfrwc,tcd->frwd", views, taps, precision=HIGH)


def temporal_back(grad_long, temporal_weight, nframes):
    views = jnp.stack([grad_long[k : k + nframes] for k in range(3)])
    return jnp.einsum("kfrwd,kcd->frwc", views, temporal_weight, precision=HIGH)


def halving_scatter(blocks, axis, order):
    count = lax.axis_size(axis)
    bits = count.bit_length() - 1
    me = lax.axis_index(axis)
    rest = blocks.shape[1:]
    blocks = blocks.reshape((2,) * bits + rest)
    for mask in order:
        dim = bits - mask.bit_length()
        bit = (me // mask) % 2
        keep = lax.dynamic_slice_in_dim(blocks, bit, 1, axis=dim)
        give = lax.dynamic_slice_in_dim(blocks, 1 - bit, 1, axis=dim)
        pairs = [(i, i ^ mask) for i in range(count)]
        blocks = keep + lax.ppermute(give, axis, pairs)
    return blocks.reshape(rest)


def doubling_sum(value, axis, first):
    count = lax.axis_size(axis)
    mask = first
    while mask < count // 2:
        pairs = [(i, i ^ mask) for i in range(count)]
        value = value + lax.ppermute(value, axis, pairs)
        mask *= 2
    ring = count // first
    pairs = [(i, first * ring_partner(i // first, ring) + i % first) for i in range(count)]
    return value + lax.ppermute(value, axis, pairs)


def ring_partner(z, ring):
    if ring % 4:
        return ring - 1 - z
    quarter = ring // 4
    shift = (3 * quarter, quarter, -quarter, -3 * quarter)
    return z + shift[z // quarter]


def pair_gather(value, axis):
    count = lax.axis_size(axis)
    low = lax.axis_index(axis) % 2 == 0
    other = lax.ppermute(value, axis, [(i, i ^ 1) for i in range(count)])
    return jnp.where(low, jnp.concatenate([value, other]), jnp.concatenate([other, value]))


def per_device(images, spatial_weight, temporal_weight, cotangent):
    nframes, strip, width, chans = images.shape
    padded = widen(padded_2(images, (("rows", 1),), 1))
    pre = convolve(padded, spatial_weight, strip, width)
    sig = jax.nn.sigmoid(pre)
    later = passed_along(cotangent, "frames", -1)
    grad_long = jnp.concatenate([cotangent, later], axis=0)
    dact = temporal_back(grad_long, temporal_weight, nframes)
    dpre = dact * sig * (1.0 + pre * (1.0 - sig))
    act = pre * sig
    earlier = passed_along(act, "frames", 1)
    longer = jnp.concatenate([earlier, act], axis=0)
    lagged = jnp.stack([longer[2 - k : 2 - k + nframes] for k in range(3)])
    mixed = jnp.einsum("kfrwc,kcd->frwd", lagged, temporal_weight, precision=HIGH)
    block_out = images + mixed
    total_cells = nframes * lax.axis_size("frames") * strip * lax.axis_size("rows") * width
    factor = 1.0 / math.sqrt(total_cells)
    offsets = [(i, j) for i in range(3) for j in range(3)]
    spatial_terms = jnp.einsum(
        "tfrwc,frwd->dtc", shifted(padded, offsets, strip, width), dpre, precision=HIGH
    )
    temporal_terms = jnp.einsum("kfrwc,frwd->dkc", lagged, cotangent, precision=HIGH)
    nrows = lax.axis_size("rows")
    terms = jnp.concatenate([spatial_terms, temporal_terms], axis=1) * factor
    terms = terms.reshape(nrows, 2, chans // nrows // 2, terms.shape[1], chans)
    parity = lax.axis_index("frames") % 2
    keep = lax.dynamic_index_in_dim(terms, parity, axis=1, keepdims=False)
    give = lax.dynamic_index_in_dim(terms, 1 - parity, axis=1, keepdims=False)
    nframes_all = lax.axis_size("frames")
    terms = keep + lax.ppermute(give, "frames", [(i, i ^ 1) for i in range(nframes_all)])
    terms = lax.all_to_all(terms, "rows", 0, 0, tiled=True).sum(axis=0)
    summed = pair_gather(doubling_sum(terms, "frames", 2), "frames")
    summed, dpre_late = lax.optimization_barrier((summed, dpre))
    dpre_wide = widen(padded_2(dpre_late, (("rows", 1),), 1))
    back = [(2 - i, 2 - j) for i in range(3) for j in range(3)]
    spatial_taps = spatial_weight.reshape(9, chans, chans)
    grad_images = cotangent + jnp.einsum(
        "tfrwd,tcd->frwc", shifted(dpre_wide, back, strip, width), spatial_taps, precision=HIGH
    )
    summed = jnp.transpose(summed, (1, 2, 0))
    grad_spatial = summed[:9].reshape(3, 3, chans, summed.shape[2])
    grad_temporal = summed[9:]
    return (block_out, grad_images, grad_spatial, grad_temporal)


def solution(mesh):
    return jax.shard_map(
        per_device,
        mesh=mesh,
        in_specs=(P("frames", "rows", None, None), P(), P(), P("frames", "rows", None, None)),
        out_specs=(
            P("frames", "rows", None, None),
            P("frames", "rows", None, None),
            P(None, None, None, "rows"),
            P(None, None, "rows"),
        ),
        check_vma=False,
    )
```

```python
import math

import jax
import jax.numpy as jnp
from jax import lax
from jax.sharding import PartitionSpec as P

HIGH = lax.Precision.HIGHEST


def padded_2(value, sides, width):
    for axis, dim in sides:
        count, length = (lax.axis_size(axis), value.shape[dim])
        up = [(i, (i + 1) % count) for i in range(count - 1)]
        down = [(j, i) for i, j in up]
        last = lax.slice_in_dim(value, length - width, length, axis=dim)
        leading = lax.slice_in_dim(value, 0, width, axis=dim)
        before = lax.ppermute(last, axis, up)
        after = lax.ppermute(leading, axis, down)
        value = jnp.concatenate([before, value, after], axis=dim)
    return value


def passed_along(value, axis, by):
    count = lax.axis_size(axis)
    pairs = [(i, i + by) for i in range(count) if 0 <= i + by < count]
    return lax.ppermute(value, axis, pairs)


def widen(array):
    return jnp.pad(array, ((0, 0), (0, 0), (1, 1), (0, 0)))


def shifted(source, offsets, height, width):
    return jnp.stack([source[:, i : i + height, j : j + width] for i, j in offsets])


def convolve(source, kernel, height, width):
    offsets = [(i, j) for i in range(3) for j in range(3)]
    views = shifted(source, offsets, height, width)
    taps = kernel.reshape(9, kernel.shape[2], kernel.shape[3])
    return jnp.einsum("tfrwc,tcd->frwd", views, taps, precision=HIGH)


def temporal_back(grad_long, temporal_weight, nframes):
    views = jnp.stack([grad_long[k : k + nframes] for k in range(3)])
    return jnp.einsum("kfrwd,kcd->frwc", views, temporal_weight, precision=HIGH)


def halving_scatter(blocks, axis, order):
    count = lax.axis_size(axis)
    bits = count.bit_length() - 1
    me = lax.axis_index(axis)
    rest = blocks.shape[1:]
    blocks = blocks.reshape((2,) * bits + rest)
    for mask in order:
        dim = bits - mask.bit_length()
        bit = (me // mask) % 2
        keep = lax.dynamic_slice_in_dim(blocks, bit, 1, axis=dim)
        give = lax.dynamic_slice_in_dim(blocks, 1 - bit, 1, axis=dim)
        pairs = [(i, i ^ mask) for i in range(count)]
        blocks = keep + lax.ppermute(give, axis, pairs)
    return blocks.reshape(rest)


def doubling_sum(value, axis, first):
    count = lax.axis_size(axis)
    mask = first
    while mask < count // 2:
        pairs = [(i, i ^ mask) for i in range(count)]
        value = value + lax.ppermute(value, axis, pairs)
        mask *= 2
    ring = count // first
    pairs = [(i, first * ring_partner(i // first, ring) + i % first) for i in range(count)]
    return value + lax.ppermute(value, axis, pairs)


def ring_partner(z, ring):
    if ring % 4:
        return ring - 1 - z
    quarter = ring // 4
    shift = (3 * quarter, quarter, -quarter, -3 * quarter)
    return z + shift[z // quarter]


def pair_gather(value, axis):
    count = lax.axis_size(axis)
    low = lax.axis_index(axis) % 2 == 0
    other = lax.ppermute(value, axis, [(i, i ^ 1) for i in range(count)])
    return jnp.where(low, jnp.concatenate([value, other]), jnp.concatenate([other, value]))


def reduce_terms(terms, nrows):
    chans, taps = terms.shape[0], terms.shape[1]
    terms = terms.reshape(nrows, 2, chans // nrows // 2, taps, terms.shape[2])
    parity = lax.axis_index("frames") % 2
    keep = lax.dynamic_index_in_dim(terms, parity, axis=1, keepdims=False)
    give = lax.dynamic_index_in_dim(terms, 1 - parity, axis=1, keepdims=False)
    nframes_all = lax.axis_size("frames")
    terms = keep + lax.ppermute(give, "frames", [(i, i ^ 1) for i in range(nframes_all)])
    terms = lax.all_to_all(terms, "rows", 0, 0, tiled=True).sum(axis=0)
    return pair_gather(doubling_sum(terms, "frames", 2), "frames")


def per_device(images, spatial_weight, temporal_weight, cotangent):
    nframes, strip, width, chans = images.shape
    padded = widen(padded_2(images, (("rows", 1),), 1))
    pre = convolve(padded, spatial_weight, strip, width)
    sig = jax.nn.sigmoid(pre)
    later = passed_along(cotangent, "frames", -1)
    grad_long = jnp.concatenate([cotangent, later], axis=0)
    dact = temporal_back(grad_long, temporal_weight, nframes)
    dpre = dact * sig * (1.0 + pre * (1.0 - sig))
    dpre_wide = widen(padded_2(dpre, (("rows", 1),), 1))
    act = pre * sig
    earlier = passed_along(act, "frames", 1)
    longer = jnp.concatenate([earlier, act], axis=0)
    lagged = jnp.stack([longer[2 - k : 2 - k + nframes] for k in range(3)])
    mixed = jnp.einsum("kfrwc,kcd->frwd", lagged, temporal_weight, precision=HIGH)
    block_out = images + mixed
    back = [(2 - i, 2 - j) for i in range(3) for j in range(3)]
    spatial_taps = spatial_weight.reshape(9, chans, chans)
    grad_images = cotangent + jnp.einsum(
        "tfrwd,tcd->frwc", shifted(dpre_wide, back, strip, width), spatial_taps, precision=HIGH
    )
    total_cells = nframes * lax.axis_size("frames") * strip * lax.axis_size("rows") * width
    factor = 1.0 / math.sqrt(total_cells)
    offsets = [(i, j) for i in range(3) for j in range(3)]
    spatial_terms = jnp.einsum(
        "tfrwc,frwd->dtc", shifted(padded, offsets, strip, width), dpre, precision=HIGH
    )
    temporal_terms = jnp.einsum("kfrwc,frwd->dkc", lagged, cotangent, precision=HIGH)
    nrows = lax.axis_size("rows")
    terms = jnp.concatenate([spatial_terms, temporal_terms], axis=1) * factor
    half = terms.shape[1] // 2
    summed = jnp.concatenate(
        [reduce_terms(terms[:, :half], nrows), reduce_terms(terms[:, half:], nrows)], axis=1
    )
    summed = jnp.transpose(summed, (1, 2, 0))
    grad_spatial = summed[:9].reshape(3, 3, chans, summed.shape[2])
    grad_temporal = summed[9:]
    return (block_out, grad_images, grad_spatial, grad_temporal)


def solution(mesh):
    return jax.shard_map(
        per_device,
        mesh=mesh,
        in_specs=(P("frames", "rows", None, None), P(), P(), P("frames", "rows", None, None)),
        out_specs=(
            P("frames", "rows", None, None),
            P("frames", "rows", None, None),
            P(None, None, None, "rows"),
            P(None, None, "rows"),
        ),
        check_vma=False,
    )
```

```python
import math

import jax
import jax.numpy as jnp
from jax import lax
from jax.sharding import PartitionSpec as P

HIGH = lax.Precision.HIGH


def padded_2(value, sides, width):
    for axis, dim in sides:
        count, length = (lax.axis_size(axis), value.shape[dim])
        up = [(i, (i + 1) % count) for i in range(count - 1)]
        down = [(j, i) for i, j in up]
        last = lax.slice_in_dim(value, length - width, length, axis=dim)
        leading = lax.slice_in_dim(value, 0, width, axis=dim)
        before = lax.ppermute(last, axis, up)
        after = lax.ppermute(leading, axis, down)
        value = jnp.concatenate([before, value, after], axis=dim)
    return value


def passed_along(value, axis, by):
    count = lax.axis_size(axis)
    pairs = [(i, i + by) for i in range(count) if 0 <= i + by < count]
    return lax.ppermute(value, axis, pairs)


def widen(array):
    return jnp.pad(array, ((0, 0), (0, 0), (1, 1), (0, 0)))


def shifted(source, offsets, height, width):
    return jnp.stack([source[:, i : i + height, j : j + width] for i, j in offsets])


def convolve(source, kernel, height, width):
    offsets = [(i, j) for i in range(3) for j in range(3)]
    views = shifted(source, offsets, height, width)
    taps = kernel.reshape(9, kernel.shape[2], kernel.shape[3])
    return jnp.einsum("tfrwc,tcd->frwd", views, taps, precision=HIGH)


def temporal_back(grad_long, temporal_weight, nframes):
    views = jnp.stack([grad_long[k : k + nframes] for k in range(3)])
    return jnp.einsum("kfrwd,kcd->frwc", views, temporal_weight, precision=HIGH)


def halving_scatter(blocks, axis, order):
    count = lax.axis_size(axis)
    bits = count.bit_length() - 1
    me = lax.axis_index(axis)
    rest = blocks.shape[1:]
    blocks = blocks.reshape((2,) * bits + rest)
    for mask in order:
        dim = bits - mask.bit_length()
        bit = (me // mask) % 2
        keep = lax.dynamic_slice_in_dim(blocks, bit, 1, axis=dim)
        give = lax.dynamic_slice_in_dim(blocks, 1 - bit, 1, axis=dim)
        pairs = [(i, i ^ mask) for i in range(count)]
        blocks = keep + lax.ppermute(give, axis, pairs)
    return blocks.reshape(rest)


def doubling_sum(value, axis, first):
    count = lax.axis_size(axis)
    mask = first
    while mask < count // 2:
        pairs = [(i, i ^ mask) for i in range(count)]
        value = value + lax.ppermute(value, axis, pairs)
        mask *= 2
    ring = count // first
    pairs = [(i, first * ring_partner(i // first, ring) + i % first) for i in range(count)]
    return value + lax.ppermute(value, axis, pairs)


def ring_partner(z, ring):
    if ring % 4:
        return ring - 1 - z
    quarter = ring // 4
    shift = (3 * quarter, quarter, -quarter, -3 * quarter)
    return z + shift[z // quarter]


def pair_gather(value, axis):
    count = lax.axis_size(axis)
    low = lax.axis_index(axis) % 2 == 0
    other = lax.ppermute(value, axis, [(i, i ^ 1) for i in range(count)])
    return jnp.where(low, jnp.concatenate([value, other]), jnp.concatenate([other, value]))


def per_device(images, spatial_weight, temporal_weight, cotangent):
    nframes, strip, width, chans = images.shape
    padded = widen(padded_2(images, (("rows", 1),), 1))
    pre = convolve(padded, spatial_weight, strip, width)
    sig = jax.nn.sigmoid(pre)
    later = passed_along(cotangent, "frames", -1)
    grad_long = jnp.concatenate([cotangent, later], axis=0)
    dact = temporal_back(grad_long, temporal_weight, nframes)
    dpre = dact * sig * (1.0 + pre * (1.0 - sig))
    dpre_wide = widen(padded_2(dpre, (("rows", 1),), 1))
    act = pre * sig
    earlier = passed_along(act, "frames", 1)
    longer = jnp.concatenate([earlier, act], axis=0)
    lagged = jnp.stack([longer[2 - k : 2 - k + nframes] for k in range(3)])
    mixed = jnp.einsum("kfrwc,kcd->frwd", lagged, temporal_weight, precision=HIGH)
    block_out = images + mixed
    back = [(2 - i, 2 - j) for i in range(3) for j in range(3)]
    spatial_taps = spatial_weight.reshape(9, chans, chans)
    grad_images = cotangent + jnp.einsum(
        "tfrwd,tcd->frwc", shifted(dpre_wide, back, strip, width), spatial_taps, precision=HIGH
    )
    total_cells = nframes * lax.axis_size("frames") * strip * lax.axis_size("rows") * width
    factor = 1.0 / math.sqrt(total_cells)
    offsets = [(i, j) for i in range(3) for j in range(3)]
    spatial_terms = jnp.einsum(
        "tfrwc,frwd->dtc", shifted(padded, offsets, strip, width), dpre, precision=HIGH
    )
    temporal_terms = jnp.einsum("kfrwc,frwd->dkc", lagged, cotangent, precision=HIGH)
    nrows = lax.axis_size("rows")
    terms = jnp.concatenate([spatial_terms, temporal_terms], axis=1) * factor
    terms = terms.reshape(nrows, 2, chans // nrows // 2, terms.shape[1], chans)
    parity = lax.axis_index("frames") % 2
    keep = lax.dynamic_index_in_dim(terms, parity, axis=1, keepdims=False)
    give = lax.dynamic_index_in_dim(terms, 1 - parity, axis=1, keepdims=False)
    nframes_all = lax.axis_size("frames")
    terms = keep + lax.ppermute(give, "frames", [(i, i ^ 1) for i in range(nframes_all)])
    terms = lax.all_to_all(terms, "rows", 0, 0, tiled=True).sum(axis=0)
    summed = pair_gather(doubling_sum(terms, "frames", 2), "frames")
    summed = jnp.transpose(summed, (1, 2, 0))
    grad_spatial = summed[:9].reshape(3, 3, chans, summed.shape[2])
    grad_temporal = summed[9:]
    return (block_out, grad_images, grad_spatial, grad_temporal)


def solution(mesh):
    return jax.shard_map(
        per_device,
        mesh=mesh,
        in_specs=(P("frames", "rows", None, None), P(), P(), P("frames", "rows", None, None)),
        out_specs=(
            P("frames", "rows", None, None),
            P("frames", "rows", None, None),
            P(None, None, None, "rows"),
            P(None, None, "rows"),
        ),
        check_vma=False,
    )
```

```python
import math

import jax
import jax.numpy as jnp
from jax import lax
from jax.sharding import PartitionSpec as P

HIGH = lax.Precision.HIGH


def padded_2(value, sides, width):
    for axis, dim in sides:
        count, length = (lax.axis_size(axis), value.shape[dim])
        up = [(i, (i + 1) % count) for i in range(count - 1)]
        down = [(j, i) for i, j in up]
        last = lax.slice_in_dim(value, length - width, length, axis=dim)
        leading = lax.slice_in_dim(value, 0, width, axis=dim)
        before = lax.ppermute(last, axis, up)
        after = lax.ppermute(leading, axis, down)
        value = jnp.concatenate([before, value, after], axis=dim)
    return value


def passed_along(value, axis, by):
    count = lax.axis_size(axis)
    pairs = [(i, i + by) for i in range(count) if 0 <= i + by < count]
    return lax.ppermute(value, axis, pairs)


def widen(array):
    return jnp.pad(array, ((0, 0), (0, 0), (1, 1), (0, 0)))


def shifted(source, offsets, height, width):
    return jnp.stack([source[:, i : i + height, j : j + width] for i, j in offsets])


def convolve(source, kernel, height, width):
    offsets = [(i, j) for i in range(3) for j in range(3)]
    views = shifted(source, offsets, height, width)
    taps = kernel.reshape(9, kernel.shape[2], kernel.shape[3])
    return jnp.einsum("tfrwc,tcd->frwd", views, taps, precision=HIGH)


def temporal_back(grad_long, temporal_weight, nframes):
    views = jnp.stack([grad_long[k : k + nframes] for k in range(3)])
    return jnp.einsum("kfrwd,kcd->frwc", views, temporal_weight, precision=HIGH)


def halving_scatter(blocks, axis, order):
    count = lax.axis_size(axis)
    bits = count.bit_length() - 1
    me = lax.axis_index(axis)
    rest = blocks.shape[1:]
    blocks = blocks.reshape((2,) * bits + rest)
    for mask in order:
        dim = bits - mask.bit_length()
        bit = (me // mask) % 2
        keep = lax.dynamic_slice_in_dim(blocks, bit, 1, axis=dim)
        give = lax.dynamic_slice_in_dim(blocks, 1 - bit, 1, axis=dim)
        pairs = [(i, i ^ mask) for i in range(count)]
        blocks = keep + lax.ppermute(give, axis, pairs)
    return blocks.reshape(rest)


def doubling_sum(value, axis, first):
    count = lax.axis_size(axis)
    ring = count // first
    turn = [(ring // 4) * (c % 2) for c in range(first)]

    def pairs_of(partner):
        pairs = []
        for i in range(count):
            c = i % first
            place = (partner((i // first + turn[c]) % ring) - turn[c]) % ring
            pairs.append((i, first * place + c))
        return pairs

    mask = 1
    while mask < ring // 2:
        value = value + lax.ppermute(value, axis, pairs_of(lambda z, m=mask: z ^ m))
        mask *= 2
    return value + lax.ppermute(value, axis, pairs_of(lambda z: ring_partner(z, ring)))


def ring_partner(z, ring):
    if ring % 4:
        return ring - 1 - z
    quarter = ring // 4
    shift = (3 * quarter, quarter, -quarter, -3 * quarter)
    return z + shift[z // quarter]


def pair_gather(value, axis):
    count = lax.axis_size(axis)
    low = lax.axis_index(axis) % 2 == 0
    other = lax.ppermute(value, axis, [(i, i ^ 1) for i in range(count)])
    return jnp.where(low, jnp.concatenate([value, other]), jnp.concatenate([other, value]))


def per_device(images, spatial_weight, temporal_weight, cotangent):
    nframes, strip, width, chans = images.shape
    padded = widen(padded_2(images, (("rows", 1),), 1))
    pre = convolve(padded, spatial_weight, strip, width)
    sig = jax.nn.sigmoid(pre)
    later = passed_along(cotangent, "frames", -1)
    grad_long = jnp.concatenate([cotangent, later], axis=0)
    dact = temporal_back(grad_long, temporal_weight, nframes)
    dpre = dact * sig * (1.0 + pre * (1.0 - sig))
    dpre_wide = widen(padded_2(dpre, (("rows", 1),), 1))
    act = pre * sig
    earlier = passed_along(act, "frames", 1)
    longer = jnp.concatenate([earlier, act], axis=0)
    lagged = jnp.stack([longer[2 - k : 2 - k + nframes] for k in range(3)])
    mixed = jnp.einsum("kfrwc,kcd->frwd", lagged, temporal_weight, precision=HIGH)
    block_out = images + mixed
    back = [(2 - i, 2 - j) for i in range(3) for j in range(3)]
    spatial_taps = spatial_weight.reshape(9, chans, chans)
    grad_images = cotangent + jnp.einsum(
        "tfrwd,tcd->frwc", shifted(dpre_wide, back, strip, width), spatial_taps, precision=HIGH
    )
    total_cells = nframes * lax.axis_size("frames") * strip * lax.axis_size("rows") * width
    factor = 1.0 / math.sqrt(total_cells)
    offsets = [(i, j) for i in range(3) for j in range(3)]
    spatial_terms = jnp.einsum(
        "tfrwc,frwd->dtc", shifted(padded, offsets, strip, width), dpre, precision=HIGH
    )
    temporal_terms = jnp.einsum("kfrwc,frwd->dkc", lagged, cotangent, precision=HIGH)
    nrows = lax.axis_size("rows")
    terms = jnp.concatenate([spatial_terms, temporal_terms], axis=1) * factor
    terms = terms.reshape(nrows, 2, chans // nrows // 2, terms.shape[1], chans)
    parity = lax.axis_index("frames") % 2
    keep = lax.dynamic_index_in_dim(terms, parity, axis=1, keepdims=False)
    give = lax.dynamic_index_in_dim(terms, 1 - parity, axis=1, keepdims=False)
    nframes_all = lax.axis_size("frames")
    terms = keep + lax.ppermute(give, "frames", [(i, i ^ 1) for i in range(nframes_all)])
    terms = lax.all_to_all(terms, "rows", 0, 0, tiled=True).sum(axis=0)
    summed = pair_gather(doubling_sum(terms, "frames", 2), "frames")
    summed = jnp.transpose(summed, (1, 2, 0))
    grad_spatial = summed[:9].reshape(3, 3, chans, summed.shape[2])
    grad_temporal = summed[9:]
    return (block_out, grad_images, grad_spatial, grad_temporal)


def solution(mesh):
    return jax.shard_map(
        per_device,
        mesh=mesh,
        in_specs=(P("frames", "rows", None, None), P(), P(), P("frames", "rows", None, None)),
        out_specs=(
            P("frames", "rows", None, None),
            P("frames", "rows", None, None),
            P(None, None, None, "rows"),
            P(None, None, "rows"),
        ),
        check_vma=False,
    )
```

```python
import math

import jax
import jax.numpy as jnp
from jax import lax
from jax.sharding import PartitionSpec as P

HIGH = lax.Precision.HIGH


def padded_2(value, sides, width):
    for axis, dim in sides:
        count, length = (lax.axis_size(axis), value.shape[dim])
        up = [(i, (i + 1) % count) for i in range(count - 1)]
        down = [(j, i) for i, j in up]
        last = lax.slice_in_dim(value, length - width, length, axis=dim)
        leading = lax.slice_in_dim(value, 0, width, axis=dim)
        before = lax.ppermute(last, axis, up)
        after = lax.ppermute(leading, axis, down)
        value = jnp.concatenate([before, value, after], axis=dim)
    return value


def passed_along(value, axis, by):
    count = lax.axis_size(axis)
    pairs = [(i, i + by) for i in range(count) if 0 <= i + by < count]
    return lax.ppermute(value, axis, pairs)


def widen(array):
    return jnp.pad(array, ((0, 0), (0, 0), (1, 1), (0, 0)))


def shifted(source, offsets, height, width):
    return jnp.stack([source[:, i : i + height, j : j + width] for i, j in offsets])


def convolve(source, kernel, height, width):
    offsets = [(i, j) for i in range(3) for j in range(3)]
    views = shifted(source, offsets, height, width)
    taps = kernel.reshape(9, kernel.shape[2], kernel.shape[3])
    return jnp.einsum("tfrwc,tcd->frwd", views, taps, precision=HIGH)


def temporal_back(grad_long, temporal_weight, nframes):
    views = jnp.stack([grad_long[k : k + nframes] for k in range(3)])
    return jnp.einsum("kfrwd,kcd->frwc", views, temporal_weight, precision=HIGH)


def halving_scatter(blocks, axis, order):
    count = lax.axis_size(axis)
    bits = count.bit_length() - 1
    me = lax.axis_index(axis)
    rest = blocks.shape[1:]
    blocks = blocks.reshape((2,) * bits + rest)
    for mask in order:
        dim = bits - mask.bit_length()
        bit = (me // mask) % 2
        keep = lax.dynamic_slice_in_dim(blocks, bit, 1, axis=dim)
        give = lax.dynamic_slice_in_dim(blocks, 1 - bit, 1, axis=dim)
        pairs = [(i, i ^ mask) for i in range(count)]
        blocks = keep + lax.ppermute(give, axis, pairs)
    return blocks.reshape(rest)


def doubling_sum(value, axis, first):
    count = lax.axis_size(axis)
    mask = first
    while mask < count // 2:
        pairs = [(i, i ^ mask) for i in range(count)]
        value = value + lax.ppermute(value, axis, pairs)
        mask *= 2
    ring = count // first
    pairs = [(i, first * ring_partner(i // first, ring) + i % first) for i in range(count)]
    return value + lax.ppermute(value, axis, pairs)


def ring_partner(z, ring):
    if ring % 4:
        return ring - 1 - z
    quarter = ring // 4
    shift = (3 * quarter, quarter, -quarter, -3 * quarter)
    return z + shift[z // quarter]


def pair_gather(value, axis):
    count = lax.axis_size(axis)
    low = lax.axis_index(axis) % 2 == 0
    other = lax.ppermute(value, axis, [(i, i ^ 1) for i in range(count)])
    return jnp.where(low, jnp.concatenate([value, other]), jnp.concatenate([other, value]))


def per_device(images, spatial_weight, temporal_weight, cotangent):
    nframes, strip, width, chans = images.shape
    later = passed_along(cotangent, "frames", -1)
    count = lax.axis_size("rows")
    up = jnp.concatenate(
        [images[:, strip - 2 :], jnp.concatenate([cotangent[:, -1:], later[:, -1:]], axis=1)], axis=3
    )
    down = jnp.concatenate(
        [images[:, :2], jnp.concatenate([cotangent[:, :1], later[:, :1]], axis=1)], axis=3
    )
    before = lax.ppermute(up, "rows", [(i, i + 1) for i in range(count - 1)])
    after = lax.ppermute(down, "rows", [(i + 1, i) for i in range(count - 1)])
    padded_all = widen(jnp.concatenate([before[..., :chans], images, after[..., :chans]], axis=1))
    cot_wide = jnp.concatenate([before[:, :1, :, chans:], cotangent, after[:, :1, :, chans:]], axis=1)
    later_wide = jnp.concatenate([before[:, 1:, :, chans:], later, after[:, 1:, :, chans:]], axis=1)
    pre_wide = convolve(padded_all, spatial_weight, strip + 2, width)
    sig_wide = jax.nn.sigmoid(pre_wide)
    grad_long = jnp.concatenate([cot_wide, later_wide], axis=0)
    dact_wide = temporal_back(grad_long, temporal_weight, nframes)
    dpre_full = dact_wide * sig_wide * (1.0 + pre_wide * (1.0 - sig_wide))
    dpre_wide = widen(dpre_full)
    padded = padded_all[:, 1:-1]
    pre = pre_wide[:, 1:-1]
    sig = sig_wide[:, 1:-1]
    dpre = dpre_full[:, 1:-1]
    act = pre * sig
    earlier = passed_along(act, "frames", 1)
    longer = jnp.concatenate([earlier, act], axis=0)
    lagged = jnp.stack([longer[2 - k : 2 - k + nframes] for k in range(3)])
    mixed = jnp.einsum("kfrwc,kcd->frwd", lagged, temporal_weight, precision=HIGH)
    block_out = images + mixed
    back = [(2 - i, 2 - j) for i in range(3) for j in range(3)]
    spatial_taps = spatial_weight.reshape(9, chans, chans)
    grad_images = cotangent + jnp.einsum(
        "tfrwd,tcd->frwc", shifted(dpre_wide, back, strip, width), spatial_taps, precision=HIGH
    )
    total_cells = nframes * lax.axis_size("frames") * strip * lax.axis_size("rows") * width
    factor = 1.0 / math.sqrt(total_cells)
    offsets = [(i, j) for i in range(3) for j in range(3)]
    spatial_terms = jnp.einsum(
        "tfrwc,frwd->dtc", shifted(padded, offsets, strip, width), dpre, precision=HIGH
    )
    temporal_terms = jnp.einsum("kfrwc,frwd->dkc", lagged, cotangent, precision=HIGH)
    nrows = lax.axis_size("rows")
    terms = jnp.concatenate([spatial_terms, temporal_terms], axis=1) * factor
    terms = terms.reshape(nrows, 2, chans // nrows // 2, terms.shape[1], chans)
    parity = lax.axis_index("frames") % 2
    keep = lax.dynamic_index_in_dim(terms, parity, axis=1, keepdims=False)
    give = lax.dynamic_index_in_dim(terms, 1 - parity, axis=1, keepdims=False)
    nframes_all = lax.axis_size("frames")
    terms = keep + lax.ppermute(give, "frames", [(i, i ^ 1) for i in range(nframes_all)])
    terms = lax.all_to_all(terms, "rows", 0, 0, tiled=True).sum(axis=0)
    summed = pair_gather(doubling_sum(terms, "frames", 2), "frames")
    summed = jnp.transpose(summed, (1, 2, 0))
    grad_spatial = summed[:9].reshape(3, 3, chans, summed.shape[2])
    grad_temporal = summed[9:]
    return (block_out, grad_images, grad_spatial, grad_temporal)


def solution(mesh):
    return jax.shard_map(
        per_device,
        mesh=mesh,
        in_specs=(P("frames", "rows", None, None), P(), P(), P("frames", "rows", None, None)),
        out_specs=(
            P("frames", "rows", None, None),
            P("frames", "rows", None, None),
            P(None, None, None, "rows"),
            P(None, None, "rows"),
        ),
        check_vma=False,
    )
```

```python
import math

import jax
import jax.numpy as jnp
from jax import lax
from jax.sharding import PartitionSpec as P

HIGH = lax.Precision.HIGH


def padded_2(value, sides, width):
    for axis, dim in sides:
        count, length = (lax.axis_size(axis), value.shape[dim])
        up = [(i, (i + 1) % count) for i in range(count - 1)]
        down = [(j, i) for i, j in up]
        last = lax.slice_in_dim(value, length - width, length, axis=dim)
        leading = lax.slice_in_dim(value, 0, width, axis=dim)
        before = lax.ppermute(last, axis, up)
        after = lax.ppermute(leading, axis, down)
        value = jnp.concatenate([before, value, after], axis=dim)
    return value


def passed_along(value, axis, by):
    count = lax.axis_size(axis)
    pairs = [(i, i + by) for i in range(count) if 0 <= i + by < count]
    return lax.ppermute(value, axis, pairs)


def widen(array):
    return jnp.pad(array, ((0, 0), (0, 0), (1, 1), (0, 0)))


def shifted(source, offsets, height, width):
    return jnp.stack([source[:, i : i + height, j : j + width] for i, j in offsets])


def convolve(source, kernel, height, width):
    offsets = [(i, j) for i in range(3) for j in range(3)]
    views = shifted(source, offsets, height, width)
    taps = kernel.reshape(9, kernel.shape[2], kernel.shape[3])
    return jnp.einsum("tfrwc,tcd->frwd", views, taps, precision=HIGH)


def temporal_back(grad_long, temporal_weight, nframes):
    views = jnp.stack([grad_long[k : k + nframes] for k in range(3)])
    return jnp.einsum("kfrwd,kcd->frwc", views, temporal_weight, precision=HIGH)


def halving_scatter(blocks, axis, order):
    count = lax.axis_size(axis)
    bits = count.bit_length() - 1
    me = lax.axis_index(axis)
    rest = blocks.shape[1:]
    blocks = blocks.reshape((2,) * bits + rest)
    for mask in order:
        dim = bits - mask.bit_length()
        bit = (me // mask) % 2
        keep = lax.dynamic_slice_in_dim(blocks, bit, 1, axis=dim)
        give = lax.dynamic_slice_in_dim(blocks, 1 - bit, 1, axis=dim)
        pairs = [(i, i ^ mask) for i in range(count)]
        blocks = keep + lax.ppermute(give, axis, pairs)
    return blocks.reshape(rest)


def doubling_sum(value, axis, first):
    count = lax.axis_size(axis)
    mask = first
    while mask < count // 2:
        pairs = [(i, i ^ mask) for i in range(count)]
        value = value + lax.ppermute(value, axis, pairs)
        mask *= 2
    ring = count // first
    pairs = [(i, first * ring_partner(i // first, ring) + i % first) for i in range(count)]
    return value + lax.ppermute(value, axis, pairs)


def ring_partner(z, ring):
    if ring % 4:
        return ring - 1 - z
    quarter = ring // 4
    shift = (3 * quarter, quarter, -quarter, -3 * quarter)
    return z + shift[z // quarter]


def pair_gather(value, axis):
    count = lax.axis_size(axis)
    low = lax.axis_index(axis) % 2 == 0
    other = lax.ppermute(value, axis, [(i, i ^ 1) for i in range(count)])
    return jnp.where(low, jnp.concatenate([value, other]), jnp.concatenate([other, value]))


def per_device(images, spatial_weight, temporal_weight, cotangent):
    nframes, strip, width, chans = images.shape
    padded = widen(padded_2(images, (("rows", 1),), 1))
    pre = convolve(padded, spatial_weight, strip, width)
    sig = jax.nn.sigmoid(pre)
    later = passed_along(cotangent, "frames", -1)
    grad_long = jnp.concatenate([cotangent, later], axis=0)
    dact = temporal_back(grad_long, temporal_weight, nframes)
    dpre = dact * sig * (1.0 + pre * (1.0 - sig))
    dpre_wide = widen(padded_2(dpre, (("rows", 1),), 1))
    act = pre * sig
    earlier = passed_along(act, "frames", 1)
    longer = jnp.concatenate([earlier, act], axis=0)
    lagged = jnp.stack([longer[2 - k : 2 - k + nframes] for k in range(3)])
    mixed = jnp.einsum("kfrwc,kcd->frwd", lagged, temporal_weight, precision=HIGH)
    block_out = images + mixed
    back = [(2 - i, 2 - j) for i in range(3) for j in range(3)]
    spatial_taps = spatial_weight.reshape(9, chans, chans)
    grad_images = cotangent + jnp.einsum(
        "tfrwd,tcd->frwc", shifted(dpre_wide, back, strip, width), spatial_taps, precision=HIGH
    )
    total_cells = nframes * lax.axis_size("frames") * strip * lax.axis_size("rows") * width
    factor = 1.0 / math.sqrt(total_cells)
    offsets = [(i, j) for i in range(3) for j in range(3)]
    spatial_terms = jnp.einsum(
        "tfrwc,frwd->dtc", shifted(padded, offsets, strip, width), dpre, precision=HIGH
    )
    leading = jnp.stack([grad_long[k : k + nframes] for k in range(3)])
    temporal_terms = jnp.einsum("frwc,kfrwd->dkc", act, leading, precision=HIGH)
    nrows = lax.axis_size("rows")
    terms = jnp.concatenate([spatial_terms, temporal_terms], axis=1) * factor
    terms = terms.reshape(nrows, 2, chans // nrows // 2, terms.shape[1], chans)
    parity = lax.axis_index("frames") % 2
    keep = lax.dynamic_index_in_dim(terms, parity, axis=1, keepdims=False)
    give = lax.dynamic_index_in_dim(terms, 1 - parity, axis=1, keepdims=False)
    nframes_all = lax.axis_size("frames")
    terms = keep + lax.ppermute(give, "frames", [(i, i ^ 1) for i in range(nframes_all)])
    terms = lax.all_to_all(terms, "rows", 0, 0, tiled=True).sum(axis=0)
    summed = pair_gather(doubling_sum(terms, "frames", 2), "frames")
    summed = jnp.transpose(summed, (1, 2, 0))
    grad_spatial = summed[:9].reshape(3, 3, chans, summed.shape[2])
    grad_temporal = summed[9:]
    return (block_out, grad_images, grad_spatial, grad_temporal)


def solution(mesh):
    return jax.shard_map(
        per_device,
        mesh=mesh,
        in_specs=(P("frames", "rows", None, None), P(), P(), P("frames", "rows", None, None)),
        out_specs=(
            P("frames", "rows", None, None),
            P("frames", "rows", None, None),
            P(None, None, None, "rows"),
            P(None, None, "rows"),
        ),
        check_vma=False,
    )
```

```python
import math

import jax
import jax.numpy as jnp
from jax import lax
from jax.sharding import PartitionSpec as P

HIGH = lax.Precision.HIGH


def padded_2(value, sides, width):
    for axis, dim in sides:
        count, length = (lax.axis_size(axis), value.shape[dim])
        up = [(i, (i + 1) % count) for i in range(count - 1)]
        down = [(j, i) for i, j in up]
        last = lax.slice_in_dim(value, length - width, length, axis=dim)
        leading = lax.slice_in_dim(value, 0, width, axis=dim)
        before = lax.ppermute(last, axis, up)
        after = lax.ppermute(leading, axis, down)
        value = jnp.concatenate([before, value, after], axis=dim)
    return value


def passed_along(value, axis, by):
    count = lax.axis_size(axis)
    pairs = [(i, i + by) for i in range(count) if 0 <= i + by < count]
    return lax.ppermute(value, axis, pairs)


def widen(array):
    return jnp.pad(array, ((0, 0), (0, 0), (1, 1), (0, 0)))


def shifted(source, offsets, height, width):
    return jnp.stack([source[:, i : i + height, j : j + width] for i, j in offsets])


def convolve(source, kernel, height, width):
    offsets = [(i, j) for i in range(3) for j in range(3)]
    views = shifted(source, offsets, height, width)
    taps = kernel.reshape(9, kernel.shape[2], kernel.shape[3])
    return jnp.einsum("tfrwc,tcd->frwd", views, taps, precision=HIGH)


def temporal_back(grad_long, temporal_weight, nframes):
    views = jnp.stack([grad_long[k : k + nframes] for k in range(3)])
    return jnp.einsum("kfrwd,kcd->frwc", views, temporal_weight, precision=HIGH)


def halving_scatter(blocks, axis, order):
    count = lax.axis_size(axis)
    bits = count.bit_length() - 1
    me = lax.axis_index(axis)
    rest = blocks.shape[1:]
    blocks = blocks.reshape((2,) * bits + rest)
    for mask in order:
        dim = bits - mask.bit_length()
        bit = (me // mask) % 2
        keep = lax.dynamic_slice_in_dim(blocks, bit, 1, axis=dim)
        give = lax.dynamic_slice_in_dim(blocks, 1 - bit, 1, axis=dim)
        pairs = [(i, i ^ mask) for i in range(count)]
        blocks = keep + lax.ppermute(give, axis, pairs)
    return blocks.reshape(rest)


def doubling_sum(value, axis, first):
    count = lax.axis_size(axis)
    mask = first
    while mask < count // 2:
        pairs = [(i, i ^ mask) for i in range(count)]
        value = value + lax.ppermute(value, axis, pairs)
        mask *= 2
    ring = count // first
    pairs = [(i, first * ring_partner(i // first, ring) + i % first) for i in range(count)]
    return value + lax.ppermute(value, axis, pairs)


def ring_partner(z, ring):
    if ring % 4:
        return ring - 1 - z
    quarter = ring // 4
    shift = (3 * quarter, quarter, -quarter, -3 * quarter)
    return z + shift[z // quarter]


def pair_gather(value, axis):
    count = lax.axis_size(axis)
    low = lax.axis_index(axis) % 2 == 0
    other = lax.ppermute(value, axis, [(i, i ^ 1) for i in range(count)])
    return jnp.where(low, jnp.concatenate([value, other]), jnp.concatenate([other, value]))


def per_device(images, spatial_weight, temporal_weight, cotangent):
    nframes, strip, width, chans = images.shape
    padded = widen(padded_2(images, (("rows", 1),), 1))
    pre = convolve(padded, spatial_weight, strip, width)
    sig = jax.nn.sigmoid(pre)
    later = passed_along(cotangent, "frames", -1)
    grad_long = jnp.concatenate([cotangent, later], axis=0)
    dact = temporal_back(grad_long, temporal_weight, nframes)
    dpre = dact * sig * (1.0 + pre * (1.0 - sig))
    dpre_wide = widen(padded_2(dpre, (("rows", 1),), 1))
    act = pre * sig
    earlier = passed_along(act, "frames", 1)
    longer = jnp.concatenate([earlier, act], axis=0)
    lagged = jnp.stack([longer[2 - k : 2 - k + nframes] for k in range(3)])
    mixed = jnp.einsum("kfrwc,kcd->frwd", lagged, temporal_weight, precision=HIGH)
    block_out = images + mixed
    back = [(2 - i, 2 - j) for i in range(3) for j in range(3)]
    spatial_taps = spatial_weight.reshape(9, chans, chans)
    grad_images = cotangent + jnp.einsum(
        "tfrwd,tcd->frwc", shifted(dpre_wide, back, strip, width), spatial_taps, precision=HIGH
    )
    total_cells = nframes * lax.axis_size("frames") * strip * lax.axis_size("rows") * width
    factor = 1.0 / math.sqrt(total_cells)
    offsets = [(i, j) for i in range(3) for j in range(3)]
    spatial_terms = jnp.einsum(
        "tfrwc,frwd->dtc", shifted(padded, offsets, strip, width), dpre, precision=HIGH
    )
    temporal_terms = jnp.einsum("kfrwc,frwd->dkc", lagged, cotangent, precision=HIGH)
    nrows = lax.axis_size("rows")
    terms = jnp.concatenate([spatial_terms, temporal_terms], axis=1) * factor
    terms = terms.reshape(nrows, 2, chans // nrows // 2, terms.shape[1], chans)
    terms = lax.all_to_all(terms, "rows", 0, 0, tiled=True).sum(axis=0)
    parity = lax.axis_index("frames") % 2
    keep = lax.dynamic_index_in_dim(terms, parity, axis=0, keepdims=False)
    give = lax.dynamic_index_in_dim(terms, 1 - parity, axis=0, keepdims=False)
    nframes_all = lax.axis_size("frames")
    terms = keep + lax.ppermute(give, "frames", [(i, i ^ 1) for i in range(nframes_all)])
    summed = pair_gather(doubling_sum(terms, "frames", 2), "frames")
    summed = jnp.transpose(summed, (1, 2, 0))
    grad_spatial = summed[:9].reshape(3, 3, chans, summed.shape[2])
    grad_temporal = summed[9:]
    return (block_out, grad_images, grad_spatial, grad_temporal)


def solution(mesh):
    return jax.shard_map(
        per_device,
        mesh=mesh,
        in_specs=(P("frames", "rows", None, None), P(), P(), P("frames", "rows", None, None)),
        out_specs=(
            P("frames", "rows", None, None),
            P("frames", "rows", None, None),
            P(None, None, None, "rows"),
            P(None, None, "rows"),
        ),
        check_vma=False,
    )
```

```python
import math

import jax
import jax.numpy as jnp
from jax import lax
from jax.sharding import PartitionSpec as P

HIGH = lax.Precision.HIGH


def padded_2(value, sides, width):
    for axis, dim in sides:
        count, length = (lax.axis_size(axis), value.shape[dim])
        up = [(i, (i + 1) % count) for i in range(count - 1)]
        down = [(j, i) for i, j in up]
        last = lax.slice_in_dim(value, length - width, length, axis=dim)
        leading = lax.slice_in_dim(value, 0, width, axis=dim)
        before = lax.ppermute(last, axis, up)
        after = lax.ppermute(leading, axis, down)
        value = jnp.concatenate([before, value, after], axis=dim)
    return value


def passed_along(value, axis, by):
    count = lax.axis_size(axis)
    pairs = [(i, i + by) for i in range(count) if 0 <= i + by < count]
    return lax.ppermute(value, axis, pairs)


def widen(array):
    return jnp.pad(array, ((0, 0), (0, 0), (1, 1), (0, 0)))


def shifted(source, offsets, height, width):
    return jnp.stack([source[:, i : i + height, j : j + width] for i, j in offsets])


def convolve(source, kernel, height, width):
    offsets = [(i, j) for i in range(3) for j in range(3)]
    views = shifted(source, offsets, height, width)
    taps = kernel.reshape(9, kernel.shape[2], kernel.shape[3])
    return jnp.einsum("tfrwc,tcd->frwd", views, taps, precision=HIGH)


def temporal_back(grad_long, temporal_weight, nframes):
    views = jnp.stack([grad_long[k : k + nframes] for k in range(3)])
    return jnp.einsum("kfrwd,kcd->frwc", views, temporal_weight, precision=HIGH)


def halving_scatter(blocks, axis, order):
    count = lax.axis_size(axis)
    bits = count.bit_length() - 1
    me = lax.axis_index(axis)
    rest = blocks.shape[1:]
    blocks = blocks.reshape((2,) * bits + rest)
    for mask in order:
        dim = bits - mask.bit_length()
        bit = (me // mask) % 2
        keep = lax.dynamic_slice_in_dim(blocks, bit, 1, axis=dim)
        give = lax.dynamic_slice_in_dim(blocks, 1 - bit, 1, axis=dim)
        pairs = [(i, i ^ mask) for i in range(count)]
        blocks = keep + lax.ppermute(give, axis, pairs)
    return blocks.reshape(rest)


def doubling_sum(value, axis, first):
    count = lax.axis_size(axis)
    mask = first
    while mask < count // 2:
        pairs = [(i, i ^ mask) for i in range(count)]
        value = value + lax.ppermute(value, axis, pairs)
        mask *= 2
    ring = count // first
    pairs = [(i, first * ring_partner(i // first, ring) + i % first) for i in range(count)]
    return value + lax.ppermute(value, axis, pairs)


def ring_partner(z, ring):
    if ring % 4:
        return ring - 1 - z
    quarter = ring // 4
    shift = (3 * quarter, quarter, -quarter, -3 * quarter)
    return z + shift[z // quarter]


def pair_gather(value, axis):
    count = lax.axis_size(axis)
    low = lax.axis_index(axis) % 2 == 0
    other = lax.ppermute(value, axis, [(i, i ^ 1) for i in range(count)])
    return jnp.where(low, jnp.concatenate([value, other]), jnp.concatenate([other, value]))


def per_device(images, spatial_weight, temporal_weight, cotangent):
    nframes, strip, width, chans = images.shape
    padded = widen(padded_2(images, (("rows", 1),), 1))
    pre = convolve(padded, spatial_weight, strip, width)
    sig = jax.nn.sigmoid(pre)
    later = passed_along(cotangent, "frames", -1)
    grad_long = jnp.concatenate([cotangent, later], axis=0)
    dact = temporal_back(grad_long, temporal_weight, nframes)
    dpre = dact * sig * (1.0 + pre * (1.0 - sig))
    act = pre * sig
    earlier = passed_along(act, "frames", 1)
    longer = jnp.concatenate([earlier, act], axis=0)
    lagged = jnp.stack([longer[2 - k : 2 - k + nframes] for k in range(3)])
    mixed = jnp.einsum("kfrwc,kcd->frwd", lagged, temporal_weight, precision=HIGH)
    block_out = images + mixed
    total_cells = nframes * lax.axis_size("frames") * strip * lax.axis_size("rows") * width
    factor = 1.0 / math.sqrt(total_cells)
    offsets = [(i, j) for i in range(3) for j in range(3)]
    spatial_terms = jnp.einsum(
        "tfrwc,frwd->dtc", shifted(padded, offsets, strip, width), dpre, precision=HIGH
    )
    temporal_terms = jnp.einsum("kfrwc,frwd->dkc", lagged, cotangent, precision=HIGH)
    nrows = lax.axis_size("rows")
    terms = jnp.concatenate([spatial_terms, temporal_terms], axis=1) * factor
    terms = terms.reshape(nrows, 2, chans // nrows // 2, terms.shape[1], chans)
    parity = lax.axis_index("frames") % 2
    keep = lax.dynamic_index_in_dim(terms, parity, axis=1, keepdims=False)
    give = lax.dynamic_index_in_dim(terms, 1 - parity, axis=1, keepdims=False)
    nframes_all = lax.axis_size("frames")
    terms = keep + lax.ppermute(give, "frames", [(i, i ^ 1) for i in range(nframes_all)])
    terms = lax.all_to_all(terms, "rows", 0, 0, tiled=True)
    terms, dpre_late = lax.optimization_barrier((terms, dpre))
    terms = terms.sum(axis=0)
    dpre_wide = widen(padded_2(dpre_late, (("rows", 1),), 1))
    back = [(2 - i, 2 - j) for i in range(3) for j in range(3)]
    spatial_taps = spatial_weight.reshape(9, chans, chans)
    grad_images = cotangent + jnp.einsum(
        "tfrwd,tcd->frwc", shifted(dpre_wide, back, strip, width), spatial_taps, precision=HIGH
    )
    summed = pair_gather(doubling_sum(terms, "frames", 2), "frames")
    summed = jnp.transpose(summed, (1, 2, 0))
    grad_spatial = summed[:9].reshape(3, 3, chans, summed.shape[2])
    grad_temporal = summed[9:]
    return (block_out, grad_images, grad_spatial, grad_temporal)


def solution(mesh):
    return jax.shard_map(
        per_device,
        mesh=mesh,
        in_specs=(P("frames", "rows", None, None), P(), P(), P("frames", "rows", None, None)),
        out_specs=(
            P("frames", "rows", None, None),
            P("frames", "rows", None, None),
            P(None, None, None, "rows"),
            P(None, None, "rows"),
        ),
        check_vma=False,
    )
```

```python
import math

import jax
import jax.numpy as jnp
from jax import lax
from jax.sharding import PartitionSpec as P

HIGH = lax.Precision.HIGH


def padded_2(value, sides, width):
    for axis, dim in sides:
        count, length = (lax.axis_size(axis), value.shape[dim])
        up = [(i, (i + 1) % count) for i in range(count - 1)]
        down = [(j, i) for i, j in up]
        last = lax.slice_in_dim(value, length - width, length, axis=dim)
        leading = lax.slice_in_dim(value, 0, width, axis=dim)
        before = lax.ppermute(last, axis, up)
        after = lax.ppermute(leading, axis, down)
        value = jnp.concatenate([before, value, after], axis=dim)
    return value


def passed_along(value, axis, by):
    count = lax.axis_size(axis)
    pairs = [(i, i + by) for i in range(count) if 0 <= i + by < count]
    return lax.ppermute(value, axis, pairs)


def widen(array):
    return jnp.pad(array, ((0, 0), (0, 0), (1, 1), (0, 0)))


def shifted(source, offsets, height, width):
    return jnp.stack([source[:, i : i + height, j : j + width] for i, j in offsets])


def convolve(source, kernel, height, width):
    offsets = [(i, j) for i in range(3) for j in range(3)]
    views = shifted(source, offsets, height, width)
    taps = kernel.reshape(9, kernel.shape[2], kernel.shape[3])
    return jnp.einsum("tfrwc,tcd->frwd", views, taps, precision=HIGH)


def temporal_back(grad_long, temporal_weight, nframes):
    views = jnp.stack([grad_long[k : k + nframes] for k in range(3)])
    return jnp.einsum("kfrwd,kcd->frwc", views, temporal_weight, precision=HIGH)


def halving_scatter(blocks, axis, order):
    count = lax.axis_size(axis)
    bits = count.bit_length() - 1
    me = lax.axis_index(axis)
    rest = blocks.shape[1:]
    blocks = blocks.reshape((2,) * bits + rest)
    for mask in order:
        dim = bits - mask.bit_length()
        bit = (me // mask) % 2
        keep = lax.dynamic_slice_in_dim(blocks, bit, 1, axis=dim)
        give = lax.dynamic_slice_in_dim(blocks, 1 - bit, 1, axis=dim)
        pairs = [(i, i ^ mask) for i in range(count)]
        blocks = keep + lax.ppermute(give, axis, pairs)
    return blocks.reshape(rest)


def doubling_sum(value, axis, first):
    count = lax.axis_size(axis)
    mask = first
    while mask < count // 2:
        pairs = [(i, i ^ mask) for i in range(count)]
        value = value + lax.ppermute(value, axis, pairs)
        mask *= 2
    ring = count // first
    pairs = [(i, first * ring_partner(i // first, ring) + i % first) for i in range(count)]
    return value + lax.ppermute(value, axis, pairs)


def ring_partner(z, ring):
    if ring % 4:
        return ring - 1 - z
    quarter = ring // 4
    shift = (3 * quarter, quarter, -quarter, -3 * quarter)
    return z + shift[z // quarter]


def pair_gather(value, axis):
    count = lax.axis_size(axis)
    low = lax.axis_index(axis) % 2 == 0
    other = lax.ppermute(value, axis, [(i, i ^ 1) for i in range(count)])
    return jnp.where(low, jnp.concatenate([value, other]), jnp.concatenate([other, value]))


def per_device(images, spatial_weight, temporal_weight, cotangent):
    nframes, strip, width, chans = images.shape
    padded = widen(padded_2(images, (("rows", 1),), 1))
    pre = convolve(padded, spatial_weight, strip, width)
    sig = jax.nn.sigmoid(pre)
    later = passed_along(cotangent, "frames", -1)
    grad_long = jnp.concatenate([cotangent, later], axis=0)
    dact = temporal_back(grad_long, temporal_weight, nframes)
    dpre = dact * sig * (1.0 + pre * (1.0 - sig))
    act = pre * sig
    total_cells = nframes * lax.axis_size("frames") * strip * lax.axis_size("rows") * width
    factor = 1.0 / math.sqrt(total_cells)
    offsets = [(i, j) for i in range(3) for j in range(3)]
    spatial_terms = jnp.einsum(
        "tfrwc,frwd->dtc", shifted(padded, offsets, strip, width), dpre, precision=HIGH
    )
    leading = jnp.stack([grad_long[k : k + nframes] for k in range(3)])
    temporal_terms = jnp.einsum("frwc,kfrwd->dkc", act, leading, precision=HIGH)
    nrows = lax.axis_size("rows")
    terms = jnp.concatenate([spatial_terms, temporal_terms], axis=1) * factor
    terms = terms.reshape(nrows, 2, chans // nrows // 2, terms.shape[1], chans)
    parity = lax.axis_index("frames") % 2
    keep = lax.dynamic_index_in_dim(terms, parity, axis=1, keepdims=False)
    give = lax.dynamic_index_in_dim(terms, 1 - parity, axis=1, keepdims=False)
    nframes_all = lax.axis_size("frames")
    terms = keep + lax.ppermute(give, "frames", [(i, i ^ 1) for i in range(nframes_all)])
    terms = lax.all_to_all(terms, "rows", 0, 0, tiled=True)
    terms, dpre_late, act = lax.optimization_barrier((terms, dpre, act))
    earlier = passed_along(act, "frames", 1)
    longer = jnp.concatenate([earlier, act], axis=0)
    lagged = jnp.stack([longer[2 - k : 2 - k + nframes] for k in range(3)])
    mixed = jnp.einsum("kfrwc,kcd->frwd", lagged, temporal_weight, precision=HIGH)
    block_out = images + mixed
    terms = terms.sum(axis=0)
    dpre_wide = widen(padded_2(dpre_late, (("rows", 1),), 1))
    back = [(2 - i, 2 - j) for i in range(3) for j in range(3)]
    spatial_taps = spatial_weight.reshape(9, chans, chans)
    grad_images = cotangent + jnp.einsum(
        "tfrwd,tcd->frwc", shifted(dpre_wide, back, strip, width), spatial_taps, precision=HIGH
    )
    summed = pair_gather(doubling_sum(terms, "frames", 2), "frames")
    summed = jnp.transpose(summed, (1, 2, 0))
    grad_spatial = summed[:9].reshape(3, 3, chans, summed.shape[2])
    grad_temporal = summed[9:]
    return (block_out, grad_images, grad_spatial, grad_temporal)


def solution(mesh):
    return jax.shard_map(
        per_device,
        mesh=mesh,
        in_specs=(P("frames", "rows", None, None), P(), P(), P("frames", "rows", None, None)),
        out_specs=(
            P("frames", "rows", None, None),
            P("frames", "rows", None, None),
            P(None, None, None, "rows"),
            P(None, None, "rows"),
        ),
        check_vma=False,
    )
```
